32 devices in a mesh: band: 8 (over y, x, core), date: 4 (over z).
Axes of the slice: x: 2, y: 2, z: 4, core: 2. Of those that a mesh axis runs over, the one named last changes fastest.
Arguments:
- inputs: bfloat16 [8, 32, 128, 512], P('date', 'band'), may hold values from -6 to 6
- preact_one: bfloat16 [8, 32, 128, 512], P('date', 'band'), may hold values from -8 to 8
- preact_two: bfloat16 [8, 32, 128, 512], P('date', 'band'), may hold values from -8 to 8
- cotangent: bfloat16 [8, 32, 128, 512], P('date', 'band'), may hold values from -6 to 6
- weight_one: bfloat16 [3, 3, 512, 512], replicated, may hold values from -0.09375 to 0.09375
- weight_two: bfloat16 [3, 3, 512, 512], replicated, may hold values from -0.09375 to 0.09375
Outputs:
- input_grad: bfloat16 [8, 32, 128, 512], P('date', 'band')
- weight_grad_one: float32 [4608, 512], P('date')
- weight_grad_two: float32 [4608, 512], P('date')
The draws below stay inside these ranges and needn't reach their ends.
All inputs are finite; a program needn't handle non-finite values.
Results may differ from the reference program's by a relative error of at most 0.0057.
Values may be sent and summed in bfloat16 or wider, within the bound.
No kernel may reach another device: no remote copies, remote signals or barrier semaphores. Data moves between devices by JAX's collectives and lax.ppermute only.
A program may use at most 128 MiB of HBM per device.

```python
import jax
import jax.numpy as jnp
from jax import lax

C = 512
LON = 128
DATES = 8
LAT = 32


def block_levels(rng, shape, split, least, top_value):
    level = 1.0
    for axis_at, blocks in split:
        draws = jax.random.uniform(jax.random.fold_in(jax.random.fold_in(rng, 6), axis_at), (blocks,), jnp.float32, least / len(split), top_value / len(split))
        level = level * jnp.repeat(jnp.exp(draws), shape[axis_at] // blocks).reshape((-1,) + (1,) * (len(shape) - 1 - axis_at))
    return level


def scatter_about(key, extent, scale, most, cuts=(), held_as=jnp.bfloat16):
    values = jax.random.normal(key, extent, jnp.float32) * scale
    if len(cuts) > 0:
        values = block_levels(key, extent, cuts, -0.22, 0.18) * values
    return jnp.clip(values, min=-most, max=most).astype(held_as)


def setup_inputs(seed: int = 0) -> dict:
    splits = jax.random.split(jax.random.key(seed), 7)
    inputs = scatter_about(splits[0], (DATES, LAT, LON, C), 1.0, 6.0, ((0, 4), (1, 8)))
    preact_one = scatter_about(splits[1], (DATES, LAT, LON, C), 2.0, 8.0, ((0, 4), (1, 8)))
    preact_two = scatter_about(splits[2], (DATES, LAT, LON, C), 2.0, 8.0, ((0, 4), (1, 8)))
    cotangent = scatter_about(splits[3], (DATES, LAT, LON, C), 1.0, 6.0, ((0, 4), (1, 8)))
    weight_one = scatter_about(splits[4], (3, 3, C, C), (9 * C) ** -0.5, 0.09375)
    weight_two = scatter_about(splits[5], (3, 3, C, C), (9 * C) ** -0.5, 0.09375)
    return {"inputs": inputs, "preact_one": preact_one, "preact_two": preact_two, "cotangent": cotangent, "weight_one": weight_one, "weight_two": weight_two}


def slope(field_value):
    logistic = jax.nn.sigmoid(field_value)
    return logistic * (1.0 + field_value * (1.0 - logistic))

def shifted(padded, row_offset, col_offset):
    return padded[:, 1 - row_offset:1 - row_offset + LAT, 1 - col_offset:1 - col_offset + LON, :]

def pad_both(field_value):
    return jnp.pad(field_value.astype(jnp.float32), ((0, 0), (1, 1), (1, 1), (0, 0)))

def weight_grad(left_field, padded):
    tap_list = []
    for row_offset in (-1, 0, 1):
        for col_offset in (-1, 0, 1):
            shifted_piece = shifted(padded, row_offset, col_offset)
            tap_list.append(lax.dot_general(left_field, shifted_piece, (((0, 1, 2), (0, 1, 2)), ((), ())), precision=lax.Precision.HIGHEST, preferred_element_type=jnp.float32))
    stacked = jnp.stack(tap_list)
    return stacked.reshape(9 * C, C) / DATES

def back_grad(padded, weight):
    accumulated = jnp.zeros((DATES, LAT, LON, C), jnp.float32)
    for row_offset in (-1, 0, 1):
        for col_offset in (-1, 0, 1):
            shifted_piece = shifted(padded, row_offset, col_offset)
            accumulated = accumulated + lax.dot_general(shifted_piece, weight[row_offset + 1, col_offset + 1], (((3,), (1,)), ((), ())), precision=lax.Precision.HIGHEST, preferred_element_type=jnp.float32)
    return accumulated

def reference(inputs, preact_one, preact_two, cotangent, weight_one, weight_two):
    act_one = jax.nn.silu(preact_one.astype(jnp.float32)).astype(jnp.bfloat16)
    delta_two = (cotangent.astype(jnp.float32) * slope(preact_two.astype(jnp.float32))).astype(jnp.bfloat16)
    padded_two = pad_both(delta_two)
    grad_two = weight_grad(act_one.astype(jnp.float32), padded_two)
    back_one = back_grad(padded_two, weight_two.astype(jnp.float32))
    delta_one = (back_one * slope(preact_one.astype(jnp.float32))).astype(jnp.bfloat16)
    padded_one = pad_both(delta_one)
    grad_one = weight_grad(inputs.astype(jnp.float32), padded_one)
    input_grad = back_grad(padded_one, weight_one.astype(jnp.float32)).astype(jnp.bfloat16)
    return (input_grad, grad_one, grad_two)
```

```python
import jax
import jax.numpy as jnp
from jax import lax
from jax.sharding import PartitionSpec as P


def extended(array, sides, width):
    for axis, dim in sides:
        peers, length = (lax.axis_size(axis), array.shape[dim])
        up = [(i, (i + 1) % peers) for i in range(peers - 1)]
        down = [(j, i) for i, j in up]
        last = lax.slice_in_dim(array, length - width, length, axis=dim)
        leading = lax.slice_in_dim(array, 0, width, axis=dim)
        before = lax.ppermute(last, axis, up)
        after = lax.ppermute(leading, axis, down)
        array = jnp.concatenate([before, array, after], axis=dim)
    return array


def slope(field_value):
    logistic = jax.nn.sigmoid(field_value)
    return logistic * (1.0 + field_value * (1.0 - logistic))


def pad_columns(field_value):
    return jnp.pad(field_value, ((0, 0), (0, 0), (1, 1), (0, 0)))


def shifted(padded, row_offset, col_offset, row_count, rim_start):
    col_count = padded.shape[2] - 2
    return padded[
        :,
        rim_start - row_offset : rim_start - row_offset + row_count,
        1 - col_offset : 1 - col_offset + col_count,
        :,
    ]


def weight_terms(left_field, padded, rim_start, grad_scale):
    row_count = left_field.shape[1]
    tap_list = []
    for row_offset in (-1, 0, 1):
        for col_offset in (-1, 0, 1):
            shifted_piece = shifted(padded, row_offset, col_offset, row_count, rim_start)
            tap_list.append(
                lax.dot_general(
                    left_field,
                    shifted_piece,
                    (((0, 1, 2), (0, 1, 2)), ((), ())),
                    preferred_element_type=jnp.float32,
                )
            )
    stacked = jnp.stack(tap_list)
    return (stacked * grad_scale).reshape(-1, stacked.shape[2])


def back_terms(padded, weight, row_count, rim_start):
    accumulated = None
    for row_offset in (-1, 0, 1):
        for col_offset in (-1, 0, 1):
            shifted_piece = shifted(padded, row_offset, col_offset, row_count, rim_start)
            product = lax.dot_general(
                shifted_piece,
                weight[row_offset + 1, col_offset + 1],
                (((3,), (1,)), ((), ())),
                preferred_element_type=jnp.float32,
            )
            accumulated = product if accumulated is None else accumulated + product
    return accumulated


def settle(grad_term):
    dates, bands = lax.axis_size("date"), lax.axis_size("band")
    rows, cols = grad_term.shape
    piece = rows // (dates * bands)
    by_band = grad_term.reshape(dates, bands, piece, cols).swapaxes(0, 1).reshape(rows, cols)
    share = lax.psum_scatter(by_band, "band", scatter_dimension=0, tiled=True)
    share = lax.psum_scatter(share, "date", scatter_dimension=0, tiled=True)
    return lax.all_gather(share, "band", axis=0, tiled=True)


def body(inputs, preact_one, preact_two, cotangent, weight_one, weight_two):
    row_count = inputs.shape[1]
    grad_scale = 1.0 / (inputs.shape[0] * lax.axis_size("date"))
    act_one = jax.nn.silu(preact_one.astype(jnp.float32)).astype(jnp.bfloat16)
    delta_two = (cotangent.astype(jnp.float32) * slope(preact_two.astype(jnp.float32))).astype(
        jnp.bfloat16
    )
    padded_two = pad_columns(extended(delta_two, (("band", 1),), 1))
    term_two = weight_terms(act_one, padded_two, 1, grad_scale)
    grad_two = settle(term_two)
    back_one = back_terms(padded_two, weight_two, row_count, 1)
    delta_one = (back_one * slope(preact_one.astype(jnp.float32))).astype(jnp.bfloat16)
    padded_one = pad_columns(extended(delta_one, (("band", 1),), 1))
    term_one = weight_terms(inputs, padded_one, 1, grad_scale)
    grad_one = settle(term_one)
    input_grad = back_terms(padded_one, weight_one, row_count, 1).astype(jnp.bfloat16)
    return (input_grad, grad_one, grad_two)


def solution(mesh):
    placed = (
        P("date", "band", None, None),
        P("date", "band", None, None),
        P("date", "band", None, None),
        P("date", "band", None, None),
        P(),
        P(),
    )
    return jax.shard_map(
        body,
        mesh=mesh,
        in_specs=placed,
        out_specs=(P("date", "band", None, None), P("date", None), P("date", None)),
        check_vma=False,
    )
```

```python
import jax
import jax.numpy as jnp
from jax import lax
from jax.sharding import PartitionSpec as P


def extended(array, sides, width):
    for axis, dim in sides:
        peers, length = (lax.axis_size(axis), array.shape[dim])
        up = [(i, (i + 1) % peers) for i in range(peers - 1)]
        down = [(j, i) for i, j in up]
        last = lax.slice_in_dim(array, length - width, length, axis=dim)
        leading = lax.slice_in_dim(array, 0, width, axis=dim)
        before = lax.ppermute(last, axis, up)
        after = lax.ppermute(leading, axis, down)
        array = jnp.concatenate([before, array, after], axis=dim)
    return array


def slope(field_value):
    logistic = jax.nn.sigmoid(field_value)
    return logistic * (1.0 + field_value * (1.0 - logistic))


def pad_columns(field_value):
    return jnp.pad(field_value, ((0, 0), (0, 0), (1, 1), (0, 0)))


def shifted(padded, row_offset, col_offset, row_count, rim_start):
    col_count = padded.shape[2] - 2
    return padded[
        :,
        rim_start - row_offset : rim_start - row_offset + row_count,
        1 - col_offset : 1 - col_offset + col_count,
        :,
    ]


def weight_terms(left_field, padded, rim_start, grad_scale):
    row_count = left_field.shape[1]
    tap_list = []
    for row_offset in (-1, 0, 1):
        for col_offset in (-1, 0, 1):
            shifted_piece = shifted(padded, row_offset, col_offset, row_count, rim_start)
            tap_list.append(
                lax.dot_general(
                    left_field,
                    shifted_piece,
                    (((0, 1, 2), (0, 1, 2)), ((), ())),
                    preferred_element_type=jnp.float32,
                )
            )
    stacked = jnp.stack(tap_list)
    return (stacked * grad_scale).reshape(-1, stacked.shape[2])


def back_terms(padded, weight, row_count, rim_start):
    accumulated = None
    for row_offset in (-1, 0, 1):
        for col_offset in (-1, 0, 1):
            shifted_piece = shifted(padded, row_offset, col_offset, row_count, rim_start)
            product = lax.dot_general(
                shifted_piece,
                weight[row_offset + 1, col_offset + 1],
                (((3,), (1,)), ((), ())),
                preferred_element_type=jnp.float32,
            )
            accumulated = product if accumulated is None else accumulated + product
    return accumulated


def settle(grad_term):
    dates, bands = lax.axis_size("date"), lax.axis_size("band")
    rows, cols = grad_term.shape
    piece = rows // (dates * bands)
    by_band = grad_term.reshape(dates, bands, piece, cols).swapaxes(0, 1).reshape(rows, cols)
    share = lax.psum_scatter(by_band.astype(jnp.bfloat16), "band", scatter_dimension=0, tiled=True)
    share = lax.psum_scatter(share.astype(jnp.float32), "date", scatter_dimension=0, tiled=True)
    return lax.all_gather(share, "band", axis=0, tiled=True)


def body(inputs, preact_one, preact_two, cotangent, weight_one, weight_two):
    row_count = inputs.shape[1]
    grad_scale = 1.0 / (inputs.shape[0] * lax.axis_size("date"))
    act_one = jax.nn.silu(preact_one.astype(jnp.float32)).astype(jnp.bfloat16)
    delta_two = (cotangent.astype(jnp.float32) * slope(preact_two.astype(jnp.float32))).astype(
        jnp.bfloat16
    )
    padded_two = pad_columns(extended(delta_two, (("band", 1),), 1))
    term_two = weight_terms(act_one, padded_two, 1, grad_scale)
    grad_two = settle(term_two)
    back_one = back_terms(padded_two, weight_two, row_count, 1)
    delta_one = (back_one * slope(preact_one.astype(jnp.float32))).astype(jnp.bfloat16)
    padded_one = pad_columns(extended(delta_one, (("band", 1),), 1))
    term_one = weight_terms(inputs, padded_one, 1, grad_scale)
    grad_one = settle(term_one)
    input_grad = back_terms(padded_one, weight_one, row_count, 1).astype(jnp.bfloat16)
    return (input_grad, grad_one, grad_two)


def solution(mesh):
    placed = (
        P("date", "band", None, None),
        P("date", "band", None, None),
        P("date", "band", None, None),
        P("date", "band", None, None),
        P(),
        P(),
    )
    return jax.shard_map(
        body,
        mesh=mesh,
        in_specs=placed,
        out_specs=(P("date", "band", None, None), P("date", None), P("date", None)),
        check_vma=False,
    )
```

```python
import jax
import jax.numpy as jnp
from jax import lax
from jax.sharding import PartitionSpec as P


def extended(array, sides, width):
    for axis, dim in sides:
        peers, length = (lax.axis_size(axis), array.shape[dim])
        up = [(i, (i + 1) % peers) for i in range(peers - 1)]
        down = [(j, i) for i, j in up]
        last = lax.slice_in_dim(array, length - width, length, axis=dim)
        leading = lax.slice_in_dim(array, 0, width, axis=dim)
        before = lax.ppermute(last, axis, up)
        after = lax.ppermute(leading, axis, down)
        array = jnp.concatenate([before, array, after], axis=dim)
    return array


def slope(field_value):
    logistic = jax.nn.sigmoid(field_value)
    return logistic * (1.0 + field_value * (1.0 - logistic))


def pad_columns(field_value):
    return jnp.pad(field_value, ((0, 0), (0, 0), (1, 1), (0, 0)))


def shifted(padded, row_offset, col_offset, row_count, rim_start):
    col_count = padded.shape[2] - 2
    return padded[
        :,
        rim_start - row_offset : rim_start - row_offset + row_count,
        1 - col_offset : 1 - col_offset + col_count,
        :,
    ]


def weight_terms(left_field, padded, rim_start):
    row_count = left_field.shape[1]
    tap_list = []
    for row_offset in (-1, 0, 1):
        for col_offset in (-1, 0, 1):
            shifted_piece = shifted(padded, row_offset, col_offset, row_count, rim_start)
            tap_list.append(
                lax.dot_general(
                    left_field,
                    shifted_piece,
                    (((0, 1, 2), (0, 1, 2)), ((), ())),
                    preferred_element_type=jnp.float32,
                )
            )
    stacked = jnp.stack(tap_list)
    return stacked.reshape(-1, stacked.shape[2])


def back_terms(padded, weight, row_count, rim_start):
    accumulated = None
    for row_offset in (-1, 0, 1):
        for col_offset in (-1, 0, 1):
            shifted_piece = shifted(padded, row_offset, col_offset, row_count, rim_start)
            product = lax.dot_general(
                shifted_piece,
                weight[row_offset + 1, col_offset + 1],
                (((3,), (1,)), ((), ())),
                preferred_element_type=jnp.float32,
            )
            accumulated = product if accumulated is None else accumulated + product
    return accumulated


def swap(array, axis, step):
    peers = lax.axis_size(axis)
    return lax.ppermute(array, axis, [(i, i ^ step) for i in range(peers)])


def halve(blocks, axis):
    bits = lax.axis_size(axis).bit_length() - 1
    mine = lax.axis_index(axis)
    for bit in range(bits):
        dim = bits - 1 - bit
        own = (mine >> bit) & 1
        keep = lax.dynamic_index_in_dim(blocks, own, axis=dim, keepdims=False)
        give = lax.dynamic_index_in_dim(blocks, 1 - own, axis=dim, keepdims=False)
        blocks = keep + swap(give, axis, 1 << bit)
    return blocks


def double(block, axis):
    peers = lax.axis_size(axis)
    bits = peers.bit_length() - 1
    mine = lax.axis_index(axis)
    for bit in reversed(range(bits)):
        other = swap(block, axis, 1 << bit)
        low = ((mine >> bit) & 1) == 0
        first = jnp.where(low, block, other)
        second = jnp.where(low, other, block)
        block = jnp.stack([first, second], axis=0)
        if bit < bits - 1:
            order = list(range(block.ndim))
            moved = bits - 1 - bit
            order = order[1 : moved + 1] + [0] + order[moved + 1 :]
            block = block.transpose(order)
    return block


def settle(grad_term, grad_scale):
    dates, bands = lax.axis_size("date"), lax.axis_size("band")
    rows, cols = grad_term.shape
    piece = rows // (dates * bands)
    band_bits, date_bits = bands.bit_length() - 1, dates.bit_length() - 1
    blocks = grad_term.reshape((dates,) + (2,) * band_bits + (piece, cols))
    order = list(range(1, band_bits + 1)) + [0, band_bits + 1, band_bits + 2]
    blocks = halve(blocks.transpose(order), "band")
    blocks = halve(blocks.reshape((2,) * date_bits + (piece, cols)), "date")
    gathered = double(blocks * grad_scale, "band")
    return gathered.reshape(rows // dates, cols)


def body(inputs, preact_one, preact_two, cotangent, weight_one, weight_two):
    row_count = inputs.shape[1]
    grad_scale = 1.0 / (inputs.shape[0] * lax.axis_size("date"))
    act_one = jax.nn.silu(preact_one.astype(jnp.float32)).astype(jnp.bfloat16)
    delta_two = (cotangent.astype(jnp.float32) * slope(preact_two.astype(jnp.float32))).astype(
        jnp.bfloat16
    )
    padded_two = pad_columns(extended(delta_two, (("band", 1),), 1))
    term_two = weight_terms(act_one, padded_two, 1)
    grad_two = settle(term_two, grad_scale)
    back_one = back_terms(padded_two, weight_two, row_count, 1)
    delta_one = (back_one * slope(preact_one.astype(jnp.float32))).astype(jnp.bfloat16)
    padded_one = pad_columns(extended(delta_one, (("band", 1),), 1))
    term_one = weight_terms(inputs, padded_one, 1)
    grad_one = settle(term_one, grad_scale)
    input_grad = back_terms(padded_one, weight_one, row_count, 1).astype(jnp.bfloat16)
    return (input_grad, grad_one, grad_two)


def solution(mesh):
    placed = (
        P("date", "band", None, None),
        P("date", "band", None, None),
        P("date", "band", None, None),
        P("date", "band", None, None),
        P(),
        P(),
    )
    return jax.shard_map(
        body,
        mesh=mesh,
        in_specs=placed,
        out_specs=(P("date", "band", None, None), P("date", None), P("date", None)),
        check_vma=False,
    )
```

```python
import jax
import jax.numpy as jnp
from jax import lax
from jax.sharding import PartitionSpec as P


def extended(array, sides, width):
    for axis, dim in sides:
        peers, length = (lax.axis_size(axis), array.shape[dim])
        up = [(i, (i + 1) % peers) for i in range(peers - 1)]
        down = [(j, i) for i, j in up]
        last = lax.slice_in_dim(array, length - width, length, axis=dim)
        leading = lax.slice_in_dim(array, 0, width, axis=dim)
        before = lax.ppermute(last, axis, up)
        after = lax.ppermute(leading, axis, down)
        array = jnp.concatenate([before, array, after], axis=dim)
    return array


def slope(field_value):
    logistic = jax.nn.sigmoid(field_value)
    return logistic * (1.0 + field_value * (1.0 - logistic))


def pad_columns(field_value):
    return jnp.pad(field_value, ((0, 0), (0, 0), (1, 1), (0, 0)))


def shifted(padded, row_offset, col_offset, row_count, rim_start):
    col_count = padded.shape[2] - 2
    return padded[
        :,
        rim_start - row_offset : rim_start - row_offset + row_count,
        1 - col_offset : 1 - col_offset + col_count,
        :,
    ]


def weight_terms(left_field, padded, rim_start):
    row_count = left_field.shape[1]
    tap_list = []
    for row_offset in (-1, 0, 1):
        for col_offset in (-1, 0, 1):
            shifted_piece = shifted(padded, row_offset, col_offset, row_count, rim_start)
            tap_list.append(
                lax.dot_general(
                    left_field,
                    shifted_piece,
                    (((0, 1, 2), (0, 1, 2)), ((), ())),
                    preferred_element_type=jnp.float32,
                )
            )
    stacked = jnp.stack(tap_list)
    return stacked.reshape(-1, stacked.shape[2])


def back_terms(padded, weight, row_count, rim_start):
    accumulated = None
    for row_offset in (-1, 0, 1):
        for col_offset in (-1, 0, 1):
            shifted_piece = shifted(padded, row_offset, col_offset, row_count, rim_start)
            product = lax.dot_general(
                shifted_piece,
                weight[row_offset + 1, col_offset + 1],
                (((3,), (1,)), ((), ())),
                preferred_element_type=jnp.float32,
            )
            accumulated = product if accumulated is None else accumulated + product
    return accumulated


def swap(array, axis, step):
    peers = lax.axis_size(axis)
    return lax.ppermute(array, axis, [(i, i ^ step) for i in range(peers)])


def halve_step(blocks, axis, bit, dim):
    own = (lax.axis_index(axis) >> bit) & 1
    keep = lax.dynamic_index_in_dim(blocks, own, axis=dim, keepdims=False)
    give = lax.dynamic_index_in_dim(blocks, 1 - own, axis=dim, keepdims=False)
    return keep + swap(give, axis, 1 << bit)


def band_halve(blocks):
    bits = lax.axis_size("band").bit_length() - 1
    blocks = halve_step(blocks, "band", 0, 1)
    if bits == 1:
        return blocks
    half = blocks.shape[0] // 2
    parts = [(blocks[:half], list(range(1, bits))), (blocks[half:], list(range(bits - 1, 0, -1)))]
    pending = [list(range(1, bits)), list(range(1, bits))]
    for step in range(bits - 1):
        moved = []
        for (part, order), left in zip(parts, pending):
            bit = order[step]
            part = halve_step(part, "band", bit, 1 + left.index(bit))
            left.remove(bit)
            moved.append((part, order))
        parts = moved
    return jnp.concatenate([parts[0][0], parts[1][0]], axis=0)


def date_halve(blocks):
    bits = lax.axis_size("date").bit_length() - 1
    for bit in range(bits):
        blocks = halve_step(blocks, "date", bit, bits - 1 - bit)
    return blocks


def band_double(block):
    bits = lax.axis_size("band").bit_length() - 1
    mine = lax.axis_index("band")
    for bit in reversed(range(bits)):
        other = swap(block, "band", 1 << bit)
        low = ((mine >> bit) & 1) == 0
        block = jnp.stack([jnp.where(low, block, other), jnp.where(low, other, block)], axis=0)
    return block


def settle(grad_term, grad_scale):
    dates, bands = lax.axis_size("date"), lax.axis_size("band")
    rows, cols = grad_term.shape
    piece = rows // (dates * bands)
    band_bits, date_bits = bands.bit_length() - 1, dates.bit_length() - 1
    blocks = band_halve(grad_term.reshape((dates,) + (2,) * band_bits + (piece, cols)))
    blocks = date_halve(blocks.reshape((2,) * date_bits + (piece, cols)))
    gathered = band_double(blocks * grad_scale)
    return gathered.reshape(rows // dates, cols)


def body(inputs, preact_one, preact_two, cotangent, weight_one, weight_two):
    row_count = inputs.shape[1]
    grad_scale = 1.0 / (inputs.shape[0] * lax.axis_size("date"))
    act_one = jax.nn.silu(preact_one.astype(jnp.float32)).astype(jnp.bfloat16)
    delta_two = (cotangent.astype(jnp.float32) * slope(preact_two.astype(jnp.float32))).astype(
        jnp.bfloat16
    )
    padded_two = pad_columns(extended(delta_two, (("band", 1),), 1))
    term_two = weight_terms(act_one, padded_two, 1)
    grad_two = settle(term_two, grad_scale)
    back_one = back_terms(padded_two, weight_two, row_count, 1)
    delta_one = (back_one * slope(preact_one.astype(jnp.float32))).astype(jnp.bfloat16)
    padded_one = pad_columns(extended(delta_one, (("band", 1),), 1))
    term_one = weight_terms(inputs, padded_one, 1)
    grad_one = settle(term_one, grad_scale)
    input_grad = back_terms(padded_one, weight_one, row_count, 1).astype(jnp.bfloat16)
    return (input_grad, grad_one, grad_two)


def solution(mesh):
    placed = (
        P("date", "band", None, None),
        P("date", "band", None, None),
        P("date", "band", None, None),
        P("date", "band", None, None),
        P(),
        P(),
    )
    return jax.shard_map(
        body,
        mesh=mesh,
        in_specs=placed,
        out_specs=(P("date", "band", None, None), P("date", None), P("date", None)),
        check_vma=False,
    )
```

```python
import jax
import jax.numpy as jnp
from jax import lax
from jax.sharding import PartitionSpec as P


def extended(array, sides, width):
    for axis, dim in sides:
        peers, length = (lax.axis_size(axis), array.shape[dim])
        up = [(i, (i + 1) % peers) for i in range(peers - 1)]
        down = [(j, i) for i, j in up]
        last = lax.slice_in_dim(array, length - width, length, axis=dim)
        leading = lax.slice_in_dim(array, 0, width, axis=dim)
        before = lax.ppermute(last, axis, up)
        after = lax.ppermute(leading, axis, down)
        array = jnp.concatenate([before, array, after], axis=dim)
    return array


def slope(field_value):
    logistic = jax.nn.sigmoid(field_value)
    return logistic * (1.0 + field_value * (1.0 - logistic))


def pad_columns(field_value):
    return jnp.pad(field_value, ((0, 0), (0, 0), (1, 1), (0, 0)))


def shifted(padded, row_offset, col_offset, row_count, rim_start):
    col_count = padded.shape[2] - 2
    return padded[
        :,
        rim_start - row_offset : rim_start - row_offset + row_count,
        1 - col_offset : 1 - col_offset + col_count,
        :,
    ]


def weight_terms(left_field, padded, rim_start):
    row_count = left_field.shape[1]
    tap_list = []
    for row_offset in (-1, 0, 1):
        for col_offset in (-1, 0, 1):
            shifted_piece = shifted(padded, row_offset, col_offset, row_count, rim_start)
            tap_list.append(
                lax.dot_general(
                    left_field,
                    shifted_piece,
                    (((0, 1, 2), (0, 1, 2)), ((), ())),
                    preferred_element_type=jnp.float32,
                )
            )
    stacked = jnp.stack(tap_list)
    return stacked.reshape(-1, stacked.shape[2])


def back_terms(padded, weight, row_count, rim_start):
    accumulated = None
    for row_offset in (-1, 0, 1):
        for col_offset in (-1, 0, 1):
            shifted_piece = shifted(padded, row_offset, col_offset, row_count, rim_start)
            product = lax.dot_general(
                shifted_piece,
                weight[row_offset + 1, col_offset + 1],
                (((3,), (1,)), ((), ())),
                preferred_element_type=jnp.float32,
            )
            accumulated = product if accumulated is None else accumulated + product
    return accumulated


def swap(array, axis, step):
    peers = lax.axis_size(axis)
    return lax.ppermute(array, axis, [(i, i ^ step) for i in range(peers)])


def halve_step(blocks, axis, bit, dim):
    own = (lax.axis_index(axis) >> bit) & 1
    keep = lax.dynamic_index_in_dim(blocks, own, axis=dim, keepdims=False)
    give = lax.dynamic_index_in_dim(blocks, 1 - own, axis=dim, keepdims=False)
    return keep + swap(give, axis, 1 << bit)


def settle_stages(grad_scale):
    dates, bands = lax.axis_size("date"), lax.axis_size("band")
    band_bits, date_bits = bands.bit_length() - 1, dates.bit_length() - 1
    stages = []

    def start(grad_term):
        rows, cols = grad_term.shape
        piece = rows // (dates * bands)
        blocks = grad_term.reshape((dates,) + (2,) * band_bits + (piece, cols))
        return halve_step(blocks, "band", 0, 1)

    stages.append((start, True))
    orders = [list(range(1, band_bits)), list(range(band_bits - 1, 0, -1))]

    def split(blocks):
        half = blocks.shape[0] // 2
        return (blocks[:half], blocks[half:])

    if band_bits > 1:
        stages.append((split, False))
    for step in range(band_bits - 1):

        def band_step(parts, step=step):
            moved = []
            for part, order in zip(parts, orders):
                bit = order[step]
                done = order[:step]
                left = [b for b in range(1, band_bits) if b not in done]
                moved.append(halve_step(part, "band", bit, 1 + left.index(bit)))
            return tuple(moved)

        stages.append((band_step, True))
    if band_bits > 1:
        stages.append((lambda parts: jnp.concatenate(parts, axis=0), False))

    def to_dates(blocks):
        return blocks.reshape((2,) * date_bits + blocks.shape[-2:])

    stages.append((to_dates, False))
    for bit in range(date_bits):
        stages.append((lambda blocks, bit=bit: halve_step(blocks, "date", bit, date_bits - 1 - bit), True))
    stages.append((lambda block: block * grad_scale, False))
    for bit in reversed(range(band_bits)):

        def gather_step(block, bit=bit):
            other = swap(block, "band", 1 << bit)
            low = ((lax.axis_index("band") >> bit) & 1) == 0
            return jnp.stack([jnp.where(low, block, other), jnp.where(low, other, block)], axis=0)

        stages.append((gather_step, True))
    return stages


class Chain:
    def __init__(self, stages, state):
        self.stages, self.state, self.at = stages, state, 0

    def advance(self, count):
        while count > 0 and self.at < len(self.stages):
            stage, sends = self.stages[self.at]
            self.state = stage(self.state)
            self.at += 1
            count -= int(sends)

    def tie(self, value):
        self.state, value = lax.optimization_barrier((self.state, value))
        return value

    def finish(self, rows, cols):
        self.advance(len(self.stages))
        return self.state.reshape(rows, cols)


def body(inputs, preact_one, preact_two, cotangent, weight_one, weight_two):
    row_count = inputs.shape[1]
    grad_scale = 1.0 / (inputs.shape[0] * lax.axis_size("date"))
    act_one = jax.nn.silu(preact_one.astype(jnp.float32)).astype(jnp.bfloat16)
    delta_two = (cotangent.astype(jnp.float32) * slope(preact_two.astype(jnp.float32))).astype(
        jnp.bfloat16
    )
    padded_two = pad_columns(extended(delta_two, (("band", 1),), 1))
    term_two = weight_terms(act_one, padded_two, 1)
    out_rows = term_two.shape[0] // lax.axis_size("date")
    two = Chain(settle_stages(grad_scale), term_two)
    two.advance(1)
    padded_two = two.tie(padded_two)
    back_one = back_terms(padded_two, weight_two, row_count, 1)
    two.advance(2)
    back_one = two.tie(back_one)
    delta_one = (back_one * slope(preact_one.astype(jnp.float32))).astype(jnp.bfloat16)
    padded_one = pad_columns(extended(delta_one, (("band", 1),), 1))
    two.advance(1)
    padded_one = two.tie(padded_one)
    term_one = weight_terms(inputs, padded_one, 1)
    one = Chain(settle_stages(grad_scale), term_one)
    one.advance(1)
    two.advance(2)
    padded_one = two.tie(padded_one)
    input_grad = back_terms(padded_one, weight_one, row_count, 1).astype(jnp.bfloat16)
    grad_two = two.finish(out_rows, term_two.shape[1])
    grad_one = one.finish(out_rows, term_one.shape[1])
    return (input_grad, grad_one, grad_two)


def solution(mesh):
    placed = (
        P("date", "band", None, None),
        P("date", "band", None, None),
        P("date", "band", None, None),
        P("date", "band", None, None),
        P(),
        P(),
    )
    return jax.shard_map(
        body,
        mesh=mesh,
        in_specs=placed,
        out_specs=(P("date", "band", None, None), P("date", None), P("date", None)),
        check_vma=False,
    )
```

```python
import jax
import jax.numpy as jnp
from jax import lax
from jax.sharding import PartitionSpec as P


def extended(array, sides, width):
    for axis, dim in sides:
        peers, length = (lax.axis_size(axis), array.shape[dim])
        up = [(i, (i + 1) % peers) for i in range(peers - 1)]
        down = [(j, i) for i, j in up]
        last = lax.slice_in_dim(array, length - width, length, axis=dim)
        leading = lax.slice_in_dim(array, 0, width, axis=dim)
        before = lax.ppermute(last, axis, up)
        after = lax.ppermute(leading, axis, down)
        array = jnp.concatenate([before, array, after], axis=dim)
    return array


def slope(field_value):
    logistic = jax.nn.sigmoid(field_value)
    return logistic * (1.0 + field_value * (1.0 - logistic))


def pad_columns(field_value):
    return jnp.pad(field_value, ((0, 0), (0, 0), (1, 1), (0, 0)))


def shifted(padded, row_offset, col_offset, row_count, rim_start):
    col_count = padded.shape[2] - 2
    return padded[
        :,
        rim_start - row_offset : rim_start - row_offset + row_count,
        1 - col_offset : 1 - col_offset + col_count,
        :,
    ]


def weight_terms(left_field, padded, rim_start):
    row_count = left_field.shape[1]
    tap_list = []
    for row_offset in (-1, 0, 1):
        for col_offset in (-1, 0, 1):
            shifted_piece = shifted(padded, row_offset, col_offset, row_count, rim_start)
            tap_list.append(
                lax.dot_general(
                    left_field,
                    shifted_piece,
                    (((0, 1, 2), (0, 1, 2)), ((), ())),
                    preferred_element_type=jnp.float32,
                )
            )
    stacked = jnp.stack(tap_list)
    return stacked.reshape(-1, stacked.shape[2])


def back_terms(padded, weight, row_count, rim_start):
    accumulated = None
    for row_offset in (-1, 0, 1):
        for col_offset in (-1, 0, 1):
            shifted_piece = shifted(padded, row_offset, col_offset, row_count, rim_start)
            product = lax.dot_general(
                shifted_piece,
                weight[row_offset + 1, col_offset + 1],
                (((3,), (1,)), ((), ())),
                preferred_element_type=jnp.float32,
            )
            accumulated = product if accumulated is None else accumulated + product
    return accumulated


def swap(array, axis, step):
    peers = lax.axis_size(axis)
    return lax.ppermute(array, axis, [(i, i ^ step) for i in range(peers)])


def halve_step(blocks, axis, bit, dim):
    own = (lax.axis_index(axis) >> bit) & 1
    keep = lax.dynamic_index_in_dim(blocks, own, axis=dim, keepdims=False)
    give = lax.dynamic_index_in_dim(blocks, 1 - own, axis=dim, keepdims=False)
    return keep + swap(give, axis, 1 << bit)


def settle_stages(grad_scale):
    dates, bands = lax.axis_size("date"), lax.axis_size("band")
    band_bits, date_bits = bands.bit_length() - 1, dates.bit_length() - 1
    stages = []

    def start(grad_term):
        rows, cols = grad_term.shape
        piece = rows // (dates * bands)
        blocks = grad_term.reshape((dates,) + (2,) * band_bits + (piece, cols))
        return halve_step(blocks, "band", 0, 1)

    stages.append((start, True))
    orders = [list(range(1, band_bits)), list(range(band_bits - 1, 0, -1))]

    def split(blocks):
        half = blocks.shape[0] // 2
        return (blocks[:half], blocks[half:])

    if band_bits > 1:
        stages.append((split, False))
    for step in range(band_bits - 1):

        def band_step(parts, step=step):
            moved = []
            for part, order in zip(parts, orders):
                bit = order[step]
                done = order[:step]
                left = [b for b in range(1, band_bits) if b not in done]
                moved.append(halve_step(part, "band", bit, 1 + left.index(bit)))
            return tuple(moved)

        stages.append((band_step, True))
    if band_bits > 1:
        stages.append((lambda parts: jnp.concatenate(parts, axis=0), False))

    def to_dates(blocks):
        return blocks.reshape((2,) * date_bits + blocks.shape[-2:])

    stages.append((to_dates, False))
    for bit in range(date_bits):
        stages.append((lambda blocks, bit=bit: halve_step(blocks, "date", bit, date_bits - 1 - bit), True))
    stages.append((lambda block: block * grad_scale, False))
    for bit in reversed(range(band_bits)):

        def gather_step(block, bit=bit):
            other = swap(block, "band", 1 << bit)
            low = ((lax.axis_index("band") >> bit) & 1) == 0
            return jnp.stack([jnp.where(low, block, other), jnp.where(low, other, block)], axis=0)

        stages.append((gather_step, True))
    return stages


class Chain:
    def __init__(self, stages, state):
        self.stages, self.state, self.at = stages, state, 0

    def advance(self, count):
        while count > 0 and self.at < len(self.stages):
            stage, sends = self.stages[self.at]
            self.state = stage(self.state)
            self.at += 1
            count -= int(sends)

    def tie(self, value):
        self.state, value = lax.optimization_barrier((self.state, value))
        return value

    def finish(self, rows, cols):
        self.advance(len(self.stages))
        return self.state.reshape(rows, cols)


def tie_chains(first, second):
    first.state, second.state = lax.optimization_barrier((first.state, second.state))


def body(inputs, preact_one, preact_two, cotangent, weight_one, weight_two):
    row_count = inputs.shape[1]
    grad_scale = 1.0 / (inputs.shape[0] * lax.axis_size("date"))
    act_one = jax.nn.silu(preact_one.astype(jnp.float32)).astype(jnp.bfloat16)
    delta_two = (cotangent.astype(jnp.float32) * slope(preact_two.astype(jnp.float32))).astype(
        jnp.bfloat16
    )
    padded_two = pad_columns(extended(delta_two, (("band", 1),), 1))
    term_two = weight_terms(act_one, padded_two, 1)
    out_rows = term_two.shape[0] // lax.axis_size("date")
    back_one = back_terms(padded_two, weight_two, row_count, 1)
    delta_one = (back_one * slope(preact_one.astype(jnp.float32))).astype(jnp.bfloat16)
    padded_one = pad_columns(extended(delta_one, (("band", 1),), 1))
    term_one = weight_terms(inputs, padded_one, 1)
    input_grad = back_terms(padded_one, weight_one, row_count, 1).astype(jnp.bfloat16)
    band_sends = lax.axis_size("band").bit_length() - 1
    date_sends = lax.axis_size("date").bit_length() - 1
    two = Chain(settle_stages(grad_scale), term_two)
    one = Chain(settle_stages(grad_scale), term_one)
    two.advance(band_sends)
    one.advance(1)
    tie_chains(two, one)
    two.advance(date_sends)
    one.advance(band_sends - 1)
    tie_chains(two, one)
    grad_two = two.finish(out_rows, term_two.shape[1])
    grad_one = one.finish(out_rows, term_one.shape[1])
    return (input_grad, grad_one, grad_two)


def solution(mesh):
    placed = (
        P("date", "band", None, None),
        P("date", "band", None, None),
        P("date", "band", None, None),
        P("date", "band", None, None),
        P(),
        P(),
    )
    return jax.shard_map(
        body,
        mesh=mesh,
        in_specs=placed,
        out_specs=(P("date", "band", None, None), P("date", None), P("date", None)),
        check_vma=False,
    )
```

```python
import jax
import jax.numpy as jnp
from jax import lax
from jax.sharding import PartitionSpec as P


def extended(array, sides, width):
    for axis, dim in sides:
        peers, length = (lax.axis_size(axis), array.shape[dim])
        up = [(i, (i + 1) % peers) for i in range(peers - 1)]
        down = [(j, i) for i, j in up]
        last = lax.slice_in_dim(array, length - width, length, axis=dim)
        leading = lax.slice_in_dim(array, 0, width, axis=dim)
        before = lax.ppermute(last, axis, up)
        after = lax.ppermute(leading, axis, down)
        array = jnp.concatenate([before, array, after], axis=dim)
    return array


def slope(field_value):
    logistic = jax.nn.sigmoid(field_value)
    return logistic * (1.0 + field_value * (1.0 - logistic))


def pad_columns(field_value):
    return jnp.pad(field_value, ((0, 0), (0, 0), (1, 1), (0, 0)))


def shifted(padded, row_offset, col_offset, row_count, rim_start):
    col_count = padded.shape[2] - 2
    return padded[
        :,
        rim_start - row_offset : rim_start - row_offset + row_count,
        1 - col_offset : 1 - col_offset + col_count,
        :,
    ]


def weight_terms(left_field, padded, rim_start):
    row_count = left_field.shape[1]
    tap_list = []
    for row_offset in (-1, 0, 1):
        for col_offset in (-1, 0, 1):
            shifted_piece = shifted(padded, row_offset, col_offset, row_count, rim_start)
            tap_list.append(
                lax.dot_general(
                    left_field,
                    shifted_piece,
                    (((0, 1, 2), (0, 1, 2)), ((), ())),
                    preferred_element_type=jnp.float32,
                )
            )
    stacked = jnp.stack(tap_list)
    return stacked.reshape(-1, stacked.shape[2])


def back_terms(padded, weight, row_count, rim_start):
    accumulated = None
    for row_offset in (-1, 0, 1):
        for col_offset in (-1, 0, 1):
            shifted_piece = shifted(padded, row_offset, col_offset, row_count, rim_start)
            product = lax.dot_general(
                shifted_piece,
                weight[row_offset + 1, col_offset + 1],
                (((3,), (1,)), ((), ())),
                preferred_element_type=jnp.float32,
            )
            accumulated = product if accumulated is None else accumulated + product
    return accumulated


def swap(array, axis, step):
    peers = lax.axis_size(axis)
    return lax.ppermute(array, axis, [(i, i ^ step) for i in range(peers)])


def halve_step(blocks, axis, bit, dim):
    own = (lax.axis_index(axis) >> bit) & 1
    keep = lax.dynamic_index_in_dim(blocks, own, axis=dim, keepdims=False)
    give = lax.dynamic_index_in_dim(blocks, 1 - own, axis=dim, keepdims=False)
    half = give.shape[0] // 2
    if half == 0:
        return keep + swap(give, axis, 1 << bit)
    got = [swap(give[:half], axis, 1 << bit), swap(give[half:], axis, 1 << bit)]
    return keep + jnp.concatenate(got, axis=0)


def settle_stages(grad_scale):
    dates, bands = lax.axis_size("date"), lax.axis_size("band")
    band_bits, date_bits = bands.bit_length() - 1, dates.bit_length() - 1
    stages = []

    def start(grad_term):
        rows, cols = grad_term.shape
        piece = rows // (dates * bands)
        blocks = grad_term.reshape((dates,) + (2,) * band_bits + (piece, cols))
        return halve_step(blocks, "band", 0, 1)

    stages.append((start, True))
    orders = [list(range(1, band_bits)), list(range(band_bits - 1, 0, -1))]

    def split(blocks):
        half = blocks.shape[0] // 2
        return (blocks[:half], blocks[half:])

    if band_bits > 1:
        stages.append((split, False))
    for step in range(band_bits - 1):

        def band_step(parts, step=step):
            moved = []
            for part, order in zip(parts, orders):
                bit = order[step]
                done = order[:step]
                left = [b for b in range(1, band_bits) if b not in done]
                moved.append(halve_step(part, "band", bit, 1 + left.index(bit)))
            return tuple(moved)

        stages.append((band_step, True))
    if band_bits > 1:
        stages.append((lambda parts: jnp.concatenate(parts, axis=0), False))

    def to_dates(blocks):
        return blocks.reshape((2,) * date_bits + blocks.shape[-2:])

    stages.append((to_dates, False))
    for bit in range(date_bits):
        stages.append((lambda blocks, bit=bit: halve_step(blocks, "date", bit, date_bits - 1 - bit), True))
    stages.append((lambda block: block * grad_scale, False))
    for bit in reversed(range(band_bits)):

        def gather_step(block, bit=bit):
            other = swap(block, "band", 1 << bit)
            low = ((lax.axis_index("band") >> bit) & 1) == 0
            return jnp.stack([jnp.where(low, block, other), jnp.where(low, other, block)], axis=0)

        stages.append((gather_step, True))
    return stages


class Chain:
    def __init__(self, stages, state):
        self.stages, self.state, self.at = stages, state, 0

    def advance(self, count):
        while count > 0 and self.at < len(self.stages):
            stage, sends = self.stages[self.at]
            self.state = stage(self.state)
            self.at += 1
            count -= int(sends)

    def tie(self, value):
        self.state, value = lax.optimization_barrier((self.state, value))
        return value

    def finish(self, rows, cols):
        self.advance(len(self.stages))
        return self.state.reshape(rows, cols)


def tie_chains(first, second):
    first.state, second.state = lax.optimization_barrier((first.state, second.state))


def body(inputs, preact_one, preact_two, cotangent, weight_one, weight_two):
    row_count = inputs.shape[1]
    grad_scale = 1.0 / (inputs.shape[0] * lax.axis_size("date"))
    act_one = jax.nn.silu(preact_one.astype(jnp.float32)).astype(jnp.bfloat16)
    delta_two = (cotangent.astype(jnp.float32) * slope(preact_two.astype(jnp.float32))).astype(
        jnp.bfloat16
    )
    padded_two = pad_columns(extended(delta_two, (("band", 1),), 1))
    term_two = weight_terms(act_one, padded_two, 1)
    out_rows = term_two.shape[0] // lax.axis_size("date")
    back_one = back_terms(padded_two, weight_two, row_count, 1)
    delta_one = (back_one * slope(preact_one.astype(jnp.float32))).astype(jnp.bfloat16)
    padded_one = pad_columns(extended(delta_one, (("band", 1),), 1))
    term_one = weight_terms(inputs, padded_one, 1)
    input_grad = back_terms(padded_one, weight_one, row_count, 1).astype(jnp.bfloat16)
    band_sends = lax.axis_size("band").bit_length() - 1
    date_sends = lax.axis_size("date").bit_length() - 1
    two = Chain(settle_stages(grad_scale), term_two)
    one = Chain(settle_stages(grad_scale), term_one)
    two.advance(band_sends)
    one.advance(1)
    tie_chains(two, one)
    two.advance(date_sends)
    one.advance(band_sends - 1)
    tie_chains(two, one)
    grad_two = two.finish(out_rows, term_two.shape[1])
    grad_one = one.finish(out_rows, term_one.shape[1])
    return (input_grad, grad_one, grad_two)


def solution(mesh):
    placed = (
        P("date", "band", None, None),
        P("date", "band", None, None),
        P("date", "band", None, None),
        P("date", "band", None, None),
        P(),
        P(),
    )
    return jax.shard_map(
        body,
        mesh=mesh,
        in_specs=placed,
        out_specs=(P("date", "band", None, None), P("date", None), P("date", None)),
        check_vma=False,
    )
```

```python
import jax
import jax.numpy as jnp
from jax import lax
from jax.sharding import PartitionSpec as P


def extended(array, sides, width):
    for axis, dim in sides:
        peers, length = (lax.axis_size(axis), array.shape[dim])
        up = [(i, (i + 1) % peers) for i in range(peers - 1)]
        down = [(j, i) for i, j in up]
        last = lax.slice_in_dim(array, length - width, length, axis=dim)
        leading = lax.slice_in_dim(array, 0, width, axis=dim)
        before = lax.ppermute(last, axis, up)
        after = lax.ppermute(leading, axis, down)
        array = jnp.concatenate([before, array, after], axis=dim)
    return array


def slope(field_value):
    logistic = jax.nn.sigmoid(field_value)
    return logistic * (1.0 + field_value * (1.0 - logistic))


def pad_columns(field_value):
    return jnp.pad(field_value, ((0, 0), (0, 0), (1, 1), (0, 0)))


def shifted(padded, row_offset, col_offset, row_count, rim_start):
    col_count = padded.shape[2] - 2
    return padded[
        :,
        rim_start - row_offset : rim_start - row_offset + row_count,
        1 - col_offset : 1 - col_offset + col_count,
        :,
    ]


def weight_terms(left_field, padded, rim_start):
    row_count = left_field.shape[1]
    tap_list = []
    for row_offset in (-1, 0, 1):
        for col_offset in (-1, 0, 1):
            shifted_piece = shifted(padded, row_offset, col_offset, row_count, rim_start)
            tap_list.append(
                lax.dot_general(
                    left_field,
                    shifted_piece,
                    (((0, 1, 2), (0, 1, 2)), ((), ())),
                    preferred_element_type=jnp.float32,
                )
            )
    stacked = jnp.stack(tap_list)
    return stacked.reshape(-1, stacked.shape[2])


def back_terms(padded, weight, row_count, rim_start):
    accumulated = None
    for row_offset in (-1, 0, 1):
        for col_offset in (-1, 0, 1):
            shifted_piece = shifted(padded, row_offset, col_offset, row_count, rim_start)
            product = lax.dot_general(
                shifted_piece,
                weight[row_offset + 1, col_offset + 1],
                (((3,), (1,)), ((), ())),
                preferred_element_type=jnp.float32,
            )
            accumulated = product if accumulated is None else accumulated + product
    return accumulated


def swap(array, axis, step):
    peers = lax.axis_size(axis)
    return lax.ppermute(array, axis, [(i, i ^ step) for i in range(peers)])


def halve_step(blocks, axis, bit, dim):
    own = (lax.axis_index(axis) >> bit) & 1
    keep = lax.dynamic_index_in_dim(blocks, own, axis=dim, keepdims=False)
    give = lax.dynamic_index_in_dim(blocks, 1 - own, axis=dim, keepdims=False)
    half = give.shape[0] // 2
    if half == 0 or give.size * give.dtype.itemsize < 1 << 20:
        return keep + swap(give, axis, 1 << bit)
    got = [swap(give[:half], axis, 1 << bit), swap(give[half:], axis, 1 << bit)]
    return keep + jnp.concatenate(got, axis=0)


def settle_stages(grad_scale):
    dates, bands = lax.axis_size("date"), lax.axis_size("band")
    band_bits, date_bits = bands.bit_length() - 1, dates.bit_length() - 1
    stages = []

    def start(grad_term):
        rows, cols = grad_term.shape
        piece = rows // (dates * bands)
        blocks = grad_term.reshape((dates,) + (2,) * band_bits + (piece, cols))
        return halve_step(blocks, "band", 0, 1)

    stages.append((start, True))
    orders = [list(range(1, band_bits)), list(range(band_bits - 1, 0, -1))]

    def split(blocks):
        half = blocks.shape[0] // 2
        return (blocks[:half], blocks[half:])

    if band_bits > 1:
        stages.append((split, False))
    for step in range(band_bits - 1):

        def band_step(parts, step=step):
            moved = []
            for part, order in zip(parts, orders):
                bit = order[step]
                done = order[:step]
                left = [b for b in range(1, band_bits) if b not in done]
                moved.append(halve_step(part, "band", bit, 1 + left.index(bit)))
            return tuple(moved)

        stages.append((band_step, True))
    if band_bits > 1:
        stages.append((lambda parts: jnp.concatenate(parts, axis=0), False))

    def to_dates(blocks):
        return blocks.reshape((2,) * date_bits + blocks.shape[-2:])

    stages.append((to_dates, False))
    for bit in range(date_bits):
        stages.append((lambda blocks, bit=bit: halve_step(blocks, "date", bit, date_bits - 1 - bit), True))
    stages.append((lambda block: block * grad_scale, False))
    for bit in reversed(range(band_bits)):

        def gather_step(block, bit=bit):
            other = swap(block, "band", 1 << bit)
            low = ((lax.axis_index("band") >> bit) & 1) == 0
            return jnp.stack([jnp.where(low, block, other), jnp.where(low, other, block)], axis=0)

        stages.append((gather_step, True))
    return stages


class Chain:
    def __init__(self, stages, state):
        self.stages, self.state, self.at = stages, state, 0

    def advance(self, count):
        while count > 0 and self.at < len(self.stages):
            stage, sends = self.stages[self.at]
            self.state = stage(self.state)
            self.at += 1
            count -= int(sends)

    def tie(self, value):
        self.state, value = lax.optimization_barrier((self.state, value))
        return value

    def finish(self, rows, cols):
        self.advance(len(self.stages))
        return self.state.reshape(rows, cols)


def tie_chains(first, second):
    first.state, second.state = lax.optimization_barrier((first.state, second.state))


def body(inputs, preact_one, preact_two, cotangent, weight_one, weight_two):
    row_count = inputs.shape[1]
    grad_scale = 1.0 / (inputs.shape[0] * lax.axis_size("date"))
    act_one = jax.nn.silu(preact_one.astype(jnp.float32)).astype(jnp.bfloat16)
    delta_two = (cotangent.astype(jnp.float32) * slope(preact_two.astype(jnp.float32))).astype(
        jnp.bfloat16
    )
    padded_two = pad_columns(extended(delta_two, (("band", 1),), 1))
    term_two = weight_terms(act_one, padded_two, 1)
    out_rows = term_two.shape[0] // lax.axis_size("date")
    back_one = back_terms(padded_two, weight_two, row_count, 1)
    delta_one = (back_one * slope(preact_one.astype(jnp.float32))).astype(jnp.bfloat16)
    padded_one = pad_columns(extended(delta_one, (("band", 1),), 1))
    term_one = weight_terms(inputs, padded_one, 1)
    input_grad = back_terms(padded_one, weight_one, row_count, 1).astype(jnp.bfloat16)
    band_sends = lax.axis_size("band").bit_length() - 1
    date_sends = lax.axis_size("date").bit_length() - 1
    two = Chain(settle_stages(grad_scale), term_two)
    one = Chain(settle_stages(grad_scale), term_one)
    two.advance(band_sends)
    one.advance(1)
    tie_chains(two, one)
    two.advance(date_sends)
    one.advance(band_sends - 1)
    tie_chains(two, one)
    grad_two = two.finish(out_rows, term_two.shape[1])
    grad_one = one.finish(out_rows, term_one.shape[1])
    return (input_grad, grad_one, grad_two)


def solution(mesh):
    placed = (
        P("date", "band", None, None),
        P("date", "band", None, None),
        P("date", "band", None, None),
        P("date", "band", None, None),
        P(),
        P(),
    )
    return jax.shard_map(
        body,
        mesh=mesh,
        in_specs=placed,
        out_specs=(P("date", "band", None, None), P("date", None), P("date", None)),
        check_vma=False,
    )
```

```python
import jax
import jax.numpy as jnp
from jax import lax
from jax.sharding import PartitionSpec as P


def extended(array, sides, width):
    for axis, dim in sides:
        peers, length = (lax.axis_size(axis), array.shape[dim])
        up = [(i, (i + 1) % peers) for i in range(peers - 1)]
        down = [(j, i) for i, j in up]
        last = lax.slice_in_dim(array, length - width, length, axis=dim)
        leading = lax.slice_in_dim(array, 0, width, axis=dim)
        before = lax.ppermute(last, axis, up)
        after = lax.ppermute(leading, axis, down)
        array = jnp.concatenate([before, array, after], axis=dim)
    return array


def slope(field_value):
    logistic = jax.nn.sigmoid(field_value)
    return logistic * (1.0 + field_value * (1.0 - logistic))


def pad_columns(field_value):
    return jnp.pad(field_value, ((0, 0), (0, 0), (1, 1), (0, 0)))


def shifted(padded, row_offset, col_offset, row_count, rim_start):
    col_count = padded.shape[2] - 2
    return padded[
        :,
        rim_start - row_offset : rim_start - row_offset + row_count,
        1 - col_offset : 1 - col_offset + col_count,
        :,
    ]


def weight_terms(left_field, padded, rim_start):
    row_count = left_field.shape[1]
    tap_list = []
    for row_offset in (-1, 0, 1):
        for col_offset in (-1, 0, 1):
            shifted_piece = shifted(padded, row_offset, col_offset, row_count, rim_start)
            tap_list.append(
                lax.dot_general(
                    left_field,
                    shifted_piece,
                    (((0, 1, 2), (0, 1, 2)), ((), ())),
                    preferred_element_type=jnp.float32,
                )
            )
    stacked = jnp.stack(tap_list)
    return stacked.reshape(-1, stacked.shape[2])


def back_terms(padded, weight, row_count, rim_start):
    accumulated = None
    for row_offset in (-1, 0, 1):
        for col_offset in (-1, 0, 1):
            shifted_piece = shifted(padded, row_offset, col_offset, row_count, rim_start)
            product = lax.dot_general(
                shifted_piece,
                weight[row_offset + 1, col_offset + 1],
                (((3,), (1,)), ((), ())),
                preferred_element_type=jnp.float32,
            )
            accumulated = product if accumulated is None else accumulated + product
    return accumulated


def swap(array, axis, step):
    peers = lax.axis_size(axis)
    return lax.ppermute(array, axis, [(i, i ^ step) for i in range(peers)])


def halve_step(blocks, axis, bit, dim):
    own = (lax.axis_index(axis) >> bit) & 1
    keep = lax.dynamic_index_in_dim(blocks, own, axis=dim, keepdims=False)
    give = lax.dynamic_index_in_dim(blocks, 1 - own, axis=dim, keepdims=False)
    flat = give.reshape((-1,) + give.shape[-2:])
    parts = 4 if give.size * give.dtype.itemsize >= 1 << 20 else 2
    while flat.shape[0] % parts:
        parts //= 2
    if parts == 1:
        return keep + swap(give, axis, 1 << bit)
    size = flat.shape[0] // parts
    got = [swap(flat[i * size : (i + 1) * size], axis, 1 << bit) for i in range(parts)]
    return keep + jnp.concatenate(got, axis=0).reshape(give.shape)


def settle_stages(grad_scale):
    dates, bands = lax.axis_size("date"), lax.axis_size("band")
    band_bits, date_bits = bands.bit_length() - 1, dates.bit_length() - 1
    stages = []

    def start(grad_term):
        rows, cols = grad_term.shape
        piece = rows // (dates * bands)
        blocks = grad_term.reshape((dates,) + (2,) * band_bits + (piece, cols))
        return halve_step(blocks, "band", 0, 1)

    stages.append((start, True))
    orders = [list(range(1, band_bits)), list(range(band_bits - 1, 0, -1))]

    def split(blocks):
        half = blocks.shape[0] // 2
        return (blocks[:half], blocks[half:])

    if band_bits > 1:
        stages.append((split, False))
    for step in range(band_bits - 1):

        def band_step(parts, step=step):
            moved = []
            for part, order in zip(parts, orders):
                bit = order[step]
                done = order[:step]
                left = [b for b in range(1, band_bits) if b not in done]
                moved.append(halve_step(part, "band", bit, 1 + left.index(bit)))
            return tuple(moved)

        stages.append((band_step, True))
    if band_bits > 1:
        stages.append((lambda parts: jnp.concatenate(parts, axis=0), False))

    def to_dates(blocks):
        return blocks.reshape((2,) * date_bits + blocks.shape[-2:])

    stages.append((to_dates, False))
    for bit in range(date_bits):
        stages.append((lambda blocks, bit=bit: halve_step(blocks, "date", bit, date_bits - 1 - bit), True))
    stages.append((lambda block: block * grad_scale, False))
    for bit in reversed(range(band_bits)):

        def gather_step(block, bit=bit):
            other = swap(block, "band", 1 << bit)
            low = ((lax.axis_index("band") >> bit) & 1) == 0
            return jnp.stack([jnp.where(low, block, other), jnp.where(low, other, block)], axis=0)

        stages.append((gather_step, True))
    return stages


class Chain:
    def __init__(self, stages, state):
        self.stages, self.state, self.at = stages, state, 0

    def advance(self, count):
        while count > 0 and self.at < len(self.stages):
            stage, sends = self.stages[self.at]
            self.state = stage(self.state)
            self.at += 1
            count -= int(sends)

    def tie(self, value):
        self.state, value = lax.optimization_barrier((self.state, value))
        return value

    def finish(self, rows, cols):
        self.advance(len(self.stages))
        return self.state.reshape(rows, cols)


def tie_chains(first, second):
    first.state, second.state = lax.optimization_barrier((first.state, second.state))


def body(inputs, preact_one, preact_two, cotangent, weight_one, weight_two):
    row_count = inputs.shape[1]
    grad_scale = 1.0 / (inputs.shape[0] * lax.axis_size("date"))
    act_one = jax.nn.silu(preact_one.astype(jnp.float32)).astype(jnp.bfloat16)
    delta_two = (cotangent.astype(jnp.float32) * slope(preact_two.astype(jnp.float32))).astype(
        jnp.bfloat16
    )
    padded_two = pad_columns(extended(delta_two, (("band", 1),), 1))
    term_two = weight_terms(act_one, padded_two, 1)
    out_rows = term_two.shape[0] // lax.axis_size("date")
    back_one = back_terms(padded_two, weight_two, row_count, 1)
    delta_one = (back_one * slope(preact_one.astype(jnp.float32))).astype(jnp.bfloat16)
    padded_one = pad_columns(extended(delta_one, (("band", 1),), 1))
    term_one = weight_terms(inputs, padded_one, 1)
    input_grad = back_terms(padded_one, weight_one, row_count, 1).astype(jnp.bfloat16)
    band_sends = lax.axis_size("band").bit_length() - 1
    date_sends = lax.axis_size("date").bit_length() - 1
    two = Chain(settle_stages(grad_scale), term_two)
    one = Chain(settle_stages(grad_scale), term_one)
    two.advance(band_sends)
    one.advance(1)
    tie_chains(two, one)
    two.advance(date_sends)
    one.advance(band_sends - 1)
    tie_chains(two, one)
    grad_two = two.finish(out_rows, term_two.shape[1])
    grad_one = one.finish(out_rows, term_one.shape[1])
    return (input_grad, grad_one, grad_two)


def solution(mesh):
    placed = (
        P("date", "band", None, None),
        P("date", "band", None, None),
        P("date", "band", None, None),
        P("date", "band", None, None),
        P(),
        P(),
    )
    return jax.shard_map(
        body,
        mesh=mesh,
        in_specs=placed,
        out_specs=(P("date", "band", None, None), P("date", None), P("date", None)),
        check_vma=False,
    )
```

```python
import jax
import jax.numpy as jnp
from jax import lax
from jax.sharding import PartitionSpec as P


def extended(array, sides, width):
    for axis, dim in sides:
        peers, length = (lax.axis_size(axis), array.shape[dim])
        up = [(i, (i + 1) % peers) for i in range(peers - 1)]
        down = [(j, i) for i, j in up]
        last = lax.slice_in_dim(array, length - width, length, axis=dim)
        leading = lax.slice_in_dim(array, 0, width, axis=dim)
        before = lax.ppermute(last, axis, up)
        after = lax.ppermute(leading, axis, down)
        array = jnp.concatenate([before, array, after], axis=dim)
    return array


def slope(field_value):
    logistic = jax.nn.sigmoid(field_value)
    return logistic * (1.0 + field_value * (1.0 - logistic))


def pad_columns(field_value):
    return jnp.pad(field_value, ((0, 0), (0, 0), (1, 1), (0, 0)))


def shifted(padded, row_offset, col_offset, row_count, rim_start):
    col_count = padded.shape[2] - 2
    return padded[
        :,
        rim_start - row_offset : rim_start - row_offset + row_count,
        1 - col_offset : 1 - col_offset + col_count,
        :,
    ]


def weight_terms(left_field, padded, rim_start):
    row_count = left_field.shape[1]
    tap_list = []
    for row_offset in (-1, 0, 1):
        for col_offset in (-1, 0, 1):
            shifted_piece = shifted(padded, row_offset, col_offset, row_count, rim_start)
            tap_list.append(
                lax.dot_general(
                    left_field,
                    shifted_piece,
                    (((0, 1, 2), (0, 1, 2)), ((), ())),
                    preferred_element_type=jnp.float32,
                )
            )
    stacked = jnp.stack(tap_list)
    return stacked.reshape(-1, stacked.shape[2])


def back_terms(padded, weight, row_count, rim_start):
    accumulated = None
    for row_offset in (-1, 0, 1):
        for col_offset in (-1, 0, 1):
            shifted_piece = shifted(padded, row_offset, col_offset, row_count, rim_start)
            product = lax.dot_general(
                shifted_piece,
                weight[row_offset + 1, col_offset + 1],
                (((3,), (1,)), ((), ())),
                preferred_element_type=jnp.float32,
            )
            accumulated = product if accumulated is None else accumulated + product
    return accumulated


def swap(array, axis, step):
    peers = lax.axis_size(axis)
    return lax.ppermute(array, axis, [(i, i ^ step) for i in range(peers)])


def halve_step(blocks, axis, bit, dim):
    own = (lax.axis_index(axis) >> bit) & 1
    keep = lax.dynamic_index_in_dim(blocks, own, axis=dim, keepdims=False)
    give = lax.dynamic_index_in_dim(blocks, 1 - own, axis=dim, keepdims=False)
    half = give.shape[0] // 2
    if half == 0:
        return keep + swap(give, axis, 1 << bit)
    got = [swap(give[:half], axis, 1 << bit), swap(give[half:], axis, 1 << bit)]
    return keep + jnp.concatenate(got, axis=0)


def settle_stages(grad_scale):
    dates, bands = lax.axis_size("date"), lax.axis_size("band")
    band_bits, date_bits = bands.bit_length() - 1, dates.bit_length() - 1
    stages = []

    def start(grad_term):
        rows, cols = grad_term.shape
        piece = rows // (dates * bands)
        blocks = grad_term.reshape((dates,) + (2,) * band_bits + (piece, cols))
        return halve_step(blocks, "band", 0, 1)

    stages.append((start, True))
    orders = [list(range(1, band_bits)), list(range(band_bits - 1, 0, -1))]

    def split(blocks):
        half = blocks.shape[0] // 2
        return (blocks[:half], blocks[half:])

    if band_bits > 1:
        stages.append((split, False))
    for step in range(band_bits - 1):

        def band_step(parts, step=step):
            moved = []
            for part, order in zip(parts, orders):
                bit = order[step]
                done = order[:step]
                left = [b for b in range(1, band_bits) if b not in done]
                moved.append(halve_step(part, "band", bit, 1 + left.index(bit)))
            return tuple(moved)

        stages.append((band_step, True))
    if band_bits > 1:
        stages.append((lambda parts: jnp.concatenate(parts, axis=0), False))

    def to_dates(blocks):
        return blocks.reshape((2,) * date_bits + blocks.shape[-2:])

    stages.append((to_dates, False))
    for bit in range(date_bits):
        stages.append((lambda blocks, bit=bit: halve_step(blocks, "date", bit, date_bits - 1 - bit), True))
    stages.append((lambda block: block * grad_scale, False))
    for bit in reversed(range(band_bits)):

        def gather_step(block, bit=bit):
            other = swap(block, "band", 1 << bit)
            low = ((lax.axis_index("band") >> bit) & 1) == 0
            return jnp.stack([jnp.where(low, block, other), jnp.where(low, other, block)], axis=0)

        stages.append((gather_step, True))
    return stages


class Chain:
    def __init__(self, stages, state):
        self.stages, self.state, self.at = stages, state, 0

    def advance(self, count):
        while count > 0 and self.at < len(self.stages):
            stage, sends = self.stages[self.at]
            self.state = stage(self.state)
            self.at += 1
            count -= int(sends)

    def tie(self, value):
        self.state, value = lax.optimization_barrier((self.state, value))
        return value

    def finish(self, rows, cols):
        self.advance(len(self.stages))
        return self.state.reshape(rows, cols)


def tie_chains(first, second):
    first.state, second.state = lax.optimization_barrier((first.state, second.state))


def tie_chains(first, second):
    first.state, second.state = lax.optimization_barrier((first.state, second.state))


def body(inputs, preact_one, preact_two, cotangent, weight_one, weight_two):
    row_count = inputs.shape[1]
    grad_scale = 1.0 / (inputs.shape[0] * lax.axis_size("date"))
    rims = extended(jnp.stack([cotangent, preact_two, preact_one]), (("band", 2),), 2)
    cotangent_rim, preact_two_rim, preact_one_rim = rims[0], rims[1], rims[2, :, 1:-1]
    act_one = jax.nn.silu(preact_one.astype(jnp.float32)).astype(jnp.bfloat16)
    delta_two = (
        cotangent_rim.astype(jnp.float32) * slope(preact_two_rim.astype(jnp.float32))
    ).astype(jnp.bfloat16)
    padded_two = pad_columns(delta_two)
    term_two = weight_terms(act_one, padded_two, 2)
    out_rows = term_two.shape[0] // lax.axis_size("date")
    back_one = back_terms(padded_two, weight_two, row_count + 2, 1)
    delta_one = (back_one * slope(preact_one_rim.astype(jnp.float32))).astype(jnp.bfloat16)
    first_row = lax.axis_index("band") * row_count - 1
    rows = first_row + lax.broadcasted_iota(jnp.int32, (1, row_count + 2, 1, 1), 1)
    inside = (rows >= 0) & (rows < row_count * lax.axis_size("band"))
    delta_one = jnp.where(inside, delta_one, jnp.zeros_like(delta_one))
    padded_one = pad_columns(delta_one)
    term_one = weight_terms(inputs, padded_one, 1)
    input_grad = back_terms(padded_one, weight_one, row_count, 1).astype(jnp.bfloat16)
    band_sends = lax.axis_size("band").bit_length() - 1
    date_sends = lax.axis_size("date").bit_length() - 1
    two = Chain(settle_stages(grad_scale), term_two)
    one = Chain(settle_stages(grad_scale), term_one)
    two.advance(band_sends)
    one.advance(1)
    tie_chains(two, one)
    two.advance(date_sends)
    one.advance(band_sends - 1)
    tie_chains(two, one)
    grad_two = two.finish(out_rows, term_two.shape[1])
    grad_one = one.finish(out_rows, term_one.shape[1])
    return (input_grad, grad_one, grad_two)


def solution(mesh):
    placed = (
        P("date", "band", None, None),
        P("date", "band", None, None),
        P("date", "band", None, None),
        P("date", "band", None, None),
        P(),
        P(),
    )
    return jax.shard_map(
        body,
        mesh=mesh,
        in_specs=placed,
        out_specs=(P("date", "band", None, None), P("date", None), P("date", None)),
        check_vma=False,
    )
```

```python
import jax
import jax.numpy as jnp
from jax import lax
from jax.sharding import PartitionSpec as P


def extended(array, sides, width):
    for axis, dim in sides:
        peers, length = (lax.axis_size(axis), array.shape[dim])
        up = [(i, (i + 1) % peers) for i in range(peers - 1)]
        down = [(j, i) for i, j in up]
        last = lax.slice_in_dim(array, length - width, length, axis=dim)
        leading = lax.slice_in_dim(array, 0, width, axis=dim)
        before = lax.ppermute(last, axis, up)
        after = lax.ppermute(leading, axis, down)
        array = jnp.concatenate([before, array, after], axis=dim)
    return array


def slope(field_value):
    logistic = jax.nn.sigmoid(field_value)
    return logistic * (1.0 + field_value * (1.0 - logistic))


def pad_columns(field_value):
    return jnp.pad(field_value, ((0, 0), (0, 0), (1, 1), (0, 0)))


def shifted(padded, row_offset, col_offset, row_count, rim_start):
    col_count = padded.shape[2] - 2
    return padded[
        :,
        rim_start - row_offset : rim_start - row_offset + row_count,
        1 - col_offset : 1 - col_offset + col_count,
        :,
    ]


def weight_terms(left_field, padded, rim_start):
    row_count = left_field.shape[1]
    tap_list = []
    for row_offset in (-1, 0, 1):
        for col_offset in (-1, 0, 1):
            shifted_piece = shifted(padded, row_offset, col_offset, row_count, rim_start)
            tap_list.append(
                lax.dot_general(
                    left_field,
                    shifted_piece,
                    (((0, 1, 2), (0, 1, 2)), ((), ())),
                    preferred_element_type=jnp.float32,
                )
            )
    stacked = jnp.stack(tap_list)
    return stacked.reshape(-1, stacked.shape[2])


def back_terms(padded, weight, row_count, rim_start):
    accumulated = None
    for row_offset in (-1, 0, 1):
        for col_offset in (-1, 0, 1):
            shifted_piece = shifted(padded, row_offset, col_offset, row_count, rim_start)
            product = lax.dot_general(
                shifted_piece,
                weight[row_offset + 1, col_offset + 1],
                (((3,), (1,)), ((), ())),
                preferred_element_type=jnp.float32,
            )
            accumulated = product if accumulated is None else accumulated + product
    return accumulated


def swap(array, axis, step):
    peers = lax.axis_size(axis)
    return lax.ppermute(array, axis, [(i, i ^ step) for i in range(peers)])


def halve_step(blocks, axis, bit, dim):
    own = (lax.axis_index(axis) >> bit) & 1
    keep = lax.dynamic_index_in_dim(blocks, own, axis=dim, keepdims=False)
    give = lax.dynamic_index_in_dim(blocks, 1 - own, axis=dim, keepdims=False)
    half = give.shape[0] // 2
    if half == 0:
        return keep + swap(give, axis, 1 << bit)
    got = [swap(give[:half], axis, 1 << bit), swap(give[half:], axis, 1 << bit)]
    return keep + jnp.concatenate(got, axis=0)


def settle_stages(grad_scale):
    dates, bands = lax.axis_size("date"), lax.axis_size("band")
    band_bits, date_bits = bands.bit_length() - 1, dates.bit_length() - 1
    stages = []

    def start(grad_term):
        rows, cols = grad_term.shape
        piece = rows // (dates * bands)
        blocks = grad_term.reshape((dates,) + (2,) * band_bits + (piece, cols))
        return halve_step(blocks, "band", 0, 1)

    stages.append((start, True))
    orders = [list(range(1, band_bits)), list(range(band_bits - 1, 0, -1))]

    def split(blocks):
        half = blocks.shape[0] // 2
        return (blocks[:half], blocks[half:])

    if band_bits > 1:
        stages.append((split, False))
    for step in range(band_bits - 1):

        def band_step(parts, step=step):
            moved = []
            for part, order in zip(parts, orders):
                bit = order[step]
                done = order[:step]
                left = [b for b in range(1, band_bits) if b not in done]
                moved.append(halve_step(part, "band", bit, 1 + left.index(bit)))
            return tuple(moved)

        stages.append((band_step, True))
    if band_bits > 1:
        stages.append((lambda parts: jnp.concatenate(parts, axis=0), False))

    def to_dates(blocks):
        return blocks.reshape((2,) * date_bits + blocks.shape[-2:])

    stages.append((to_dates, False))
    for bit in range(date_bits):
        stages.append((lambda blocks, bit=bit: halve_step(blocks, "date", bit, date_bits - 1 - bit), True))
    stages.append((lambda block: block * grad_scale, False))
    for bit in reversed(range(band_bits)):

        def gather_step(block, bit=bit):
            other = swap(block, "band", 1 << bit)
            low = ((lax.axis_index("band") >> bit) & 1) == 0
            return jnp.stack([jnp.where(low, block, other), jnp.where(low, other, block)], axis=0)

        stages.append((gather_step, True))
    return stages


class Chain:
    def __init__(self, stages, state):
        self.stages, self.state, self.at = stages, state, 0

    def advance(self, count):
        while count > 0 and self.at < len(self.stages):
            stage, sends = self.stages[self.at]
            self.state = stage(self.state)
            self.at += 1
            count -= int(sends)

    def quiet(self):
        while self.at < len(self.stages) and not self.stages[self.at][1]:
            self.state = self.stages[self.at][0](self.state)
            self.at += 1

    def tie(self, value):
        self.state, value = lax.optimization_barrier((self.state, value))
        return value

    def finish(self, rows, cols):
        self.advance(len(self.stages))
        return self.state.reshape(rows, cols)


def tie_chains(first, second):
    first.state, second.state = lax.optimization_barrier((first.state, second.state))


def body(inputs, preact_one, preact_two, cotangent, weight_one, weight_two):
    row_count = inputs.shape[1]
    grad_scale = 1.0 / (inputs.shape[0] * lax.axis_size("date"))
    act_one = jax.nn.silu(preact_one.astype(jnp.float32)).astype(jnp.bfloat16)
    delta_two = (cotangent.astype(jnp.float32) * slope(preact_two.astype(jnp.float32))).astype(
        jnp.bfloat16
    )
    padded_two = pad_columns(extended(delta_two, (("band", 1),), 1))
    term_two = weight_terms(act_one, padded_two, 1)
    out_rows = term_two.shape[0] // lax.axis_size("date")
    back_one = back_terms(padded_two, weight_two, row_count, 1)
    delta_one = (back_one * slope(preact_one.astype(jnp.float32))).astype(jnp.bfloat16)
    padded_one = pad_columns(extended(delta_one, (("band", 1),), 1))
    term_one = weight_terms(inputs, padded_one, 1)
    input_grad = back_terms(padded_one, weight_one, row_count, 1).astype(jnp.bfloat16)
    band_sends = lax.axis_size("band").bit_length() - 1
    date_sends = lax.axis_size("date").bit_length() - 1
    two = Chain(settle_stages(grad_scale), term_two)
    one = Chain(settle_stages(grad_scale), term_one)
    two.advance(band_sends)
    one.advance(1)
    tie_chains(two, one)
    two.advance(date_sends)
    one.advance(band_sends - 1)
    tie_chains(two, one)
    two.quiet()
    bits = lax.axis_size("band").bit_length() - 1
    gathered = lax.all_gather(two.state, "band", axis=0, tiled=False)
    gathered = gathered.reshape((2,) * bits + two.state.shape)
    order = list(reversed(range(bits))) + [bits, bits + 1]
    grad_two = gathered.transpose(order).reshape(out_rows, term_two.shape[1])
    grad_one = one.finish(out_rows, term_one.shape[1])
    return (input_grad, grad_one, grad_two)


def solution(mesh):
    placed = (
        P("date", "band", None, None),
        P("date", "band", None, None),
        P("date", "band", None, None),
        P("date", "band", None, None),
        P(),
        P(),
    )
    return jax.shard_map(
        body,
        mesh=mesh,
        in_specs=placed,
        out_specs=(P("date", "band", None, None), P("date", None), P("date", None)),
        check_vma=False,
    )
```

```python
import jax
import jax.numpy as jnp
from jax import lax
from jax.sharding import PartitionSpec as P


def extended(array, sides, width):
    for axis, dim in sides:
        peers, length = (lax.axis_size(axis), array.shape[dim])
        up = [(i, (i + 1) % peers) for i in range(peers - 1)]
        down = [(j, i) for i, j in up]
        last = lax.slice_in_dim(array, length - width, length, axis=dim)
        leading = lax.slice_in_dim(array, 0, width, axis=dim)
        before = lax.ppermute(last, axis, up)
        after = lax.ppermute(leading, axis, down)
        array = jnp.concatenate([before, array, after], axis=dim)
    return array


def slope(field_value):
    logistic = jax.nn.sigmoid(field_value)
    return logistic * (1.0 + field_value * (1.0 - logistic))


def pad_columns(field_value):
    return jnp.pad(field_value, ((0, 0), (0, 0), (1, 1), (0, 0)))


def shifted(padded, row_offset, col_offset, row_count, rim_start):
    col_count = padded.shape[2] - 2
    return padded[
        :,
        rim_start - row_offset : rim_start - row_offset + row_count,
        1 - col_offset : 1 - col_offset + col_count,
        :,
    ]


def weight_terms(left_field, padded, rim_start):
    row_count = left_field.shape[1]
    tap_list = []
    for row_offset in (-1, 0, 1):
        for col_offset in (-1, 0, 1):
            shifted_piece = shifted(padded, row_offset, col_offset, row_count, rim_start)
            tap_list.append(
                lax.dot_general(
                    left_field,
                    shifted_piece,
                    (((0, 1, 2), (0, 1, 2)), ((), ())),
                    preferred_element_type=jnp.float32,
                )
            )
    stacked = jnp.stack(tap_list)
    return stacked.reshape(-1, stacked.shape[2])


def back_terms(padded, weight, row_count, rim_start):
    accumulated = None
    for row_offset in (-1, 0, 1):
        for col_offset in (-1, 0, 1):
            shifted_piece = shifted(padded, row_offset, col_offset, row_count, rim_start)
            product = lax.dot_general(
                shifted_piece,
                weight[row_offset + 1, col_offset + 1],
                (((3,), (1,)), ((), ())),
                preferred_element_type=jnp.float32,
            )
            accumulated = product if accumulated is None else accumulated + product
    return accumulated


def swap(array, axis, step):
    peers = lax.axis_size(axis)
    return lax.ppermute(array, axis, [(i, i ^ step) for i in range(peers)])


def halve_step(blocks, axis, bit, dim):
    own = (lax.axis_index(axis) >> bit) & 1
    keep = lax.dynamic_index_in_dim(blocks, own, axis=dim, keepdims=False)
    give = lax.dynamic_index_in_dim(blocks, 1 - own, axis=dim, keepdims=False)
    half = give.shape[0] // 2
    if half == 0:
        return keep + swap(give, axis, 1 << bit)
    got = [swap(give[:half], axis, 1 << bit), swap(give[half:], axis, 1 << bit)]
    return keep + jnp.concatenate(got, axis=0)


def settle_stages(grad_scale):
    dates, bands = lax.axis_size("date"), lax.axis_size("band")
    band_bits, date_bits = bands.bit_length() - 1, dates.bit_length() - 1
    stages = []

    def start(grad_term):
        rows, cols = grad_term.shape
        piece = rows // (dates * bands)
        blocks = grad_term.reshape((dates,) + (2,) * band_bits + (piece, cols))
        return halve_step(blocks, "band", 0, 1)

    stages.append((start, True))
    orders = [list(range(1, band_bits)), list(range(band_bits - 1, 0, -1))]

    def split(blocks):
        half = blocks.shape[0] // 2
        return (blocks[:half], blocks[half:])

    if band_bits > 1:
        stages.append((split, False))
    for step in range(band_bits - 1):

        def band_step(parts, step=step):
            moved = []
            for part, order in zip(parts, orders):
                bit = order[step]
                done = order[:step]
                left = [b for b in range(1, band_bits) if b not in done]
                moved.append(halve_step(part, "band", bit, 1 + left.index(bit)))
            return tuple(moved)

        stages.append((band_step, True))
    if band_bits > 1:
        stages.append((lambda parts: jnp.concatenate(parts, axis=0), False))

    def to_dates(blocks):
        return blocks.reshape((2,) * date_bits + blocks.shape[-2:])

    stages.append((to_dates, False))
    for bit in range(date_bits):
        stages.append((lambda blocks, bit=bit: halve_step(blocks, "date", bit, date_bits - 1 - bit), True))
    stages.append((lambda block: block * grad_scale, False))
    for bit in reversed(range(band_bits)):

        def gather_step(block, bit=bit):
            half = block.shape[0] // 2
            parts = [block[:half], block[half:]] if half else [block]
            other = jnp.concatenate([swap(part, "band", 1 << bit) for part in parts], axis=0)
            low = ((lax.axis_index("band") >> bit) & 1) == 0
            return jnp.stack([jnp.where(low, block, other), jnp.where(low, other, block)], axis=0)

        stages.append((gather_step, True))
    return stages


class Chain:
    def __init__(self, stages, state):
        self.stages, self.state, self.at = stages, state, 0

    def advance(self, count):
        while count > 0 and self.at < len(self.stages):
            stage, sends = self.stages[self.at]
            self.state = stage(self.state)
            self.at += 1
            count -= int(sends)

    def tie(self, value):
        self.state, value = lax.optimization_barrier((self.state, value))
        return value

    def finish(self, rows, cols):
        self.advance(len(self.stages))
        return self.state.reshape(rows, cols)


def tie_chains(first, second):
    first.state, second.state = lax.optimization_barrier((first.state, second.state))


def body(inputs, preact_one, preact_two, cotangent, weight_one, weight_two):
    row_count = inputs.shape[1]
    grad_scale = 1.0 / (inputs.shape[0] * lax.axis_size("date"))
    act_one = jax.nn.silu(preact_one.astype(jnp.float32)).astype(jnp.bfloat16)
    delta_two = (cotangent.astype(jnp.float32) * slope(preact_two.astype(jnp.float32))).astype(
        jnp.bfloat16
    )
    padded_two = pad_columns(extended(delta_two, (("band", 1),), 1))
    term_two = weight_terms(act_one, padded_two, 1)
    out_rows = term_two.shape[0] // lax.axis_size("date")
    back_one = back_terms(padded_two, weight_two, row_count, 1)
    delta_one = (back_one * slope(preact_one.astype(jnp.float32))).astype(jnp.bfloat16)
    padded_one = pad_columns(extended(delta_one, (("band", 1),), 1))
    term_one = weight_terms(inputs, padded_one, 1)
    input_grad = back_terms(padded_one, weight_one, row_count, 1).astype(jnp.bfloat16)
    band_sends = lax.axis_size("band").bit_length() - 1
    date_sends = lax.axis_size("date").bit_length() - 1
    two = Chain(settle_stages(grad_scale), term_two)
    one = Chain(settle_stages(grad_scale), term_one)
    two.advance(band_sends)
    one.advance(1)
    tie_chains(two, one)
    two.advance(date_sends)
    one.advance(band_sends - 1)
    tie_chains(two, one)
    grad_two = two.finish(out_rows, term_two.shape[1])
    grad_one = one.finish(out_rows, term_one.shape[1])
    return (input_grad, grad_one, grad_two)


def solution(mesh):
    placed = (
        P("date", "band", None, None),
        P("date", "band", None, None),
        P("date", "band", None, None),
        P("date", "band", None, None),
        P(),
        P(),
    )
    return jax.shard_map(
        body,
        mesh=mesh,
        in_specs=placed,
        out_specs=(P("date", "band", None, None), P("date", None), P("date", None)),
        check_vma=False,
    )
```

```python
import jax
import jax.numpy as jnp
from jax import lax
from jax.sharding import PartitionSpec as P


def extended(array, sides, width):
    for axis, dim in sides:
        peers, length = (lax.axis_size(axis), array.shape[dim])
        up = [(i, (i + 1) % peers) for i in range(peers - 1)]
        down = [(j, i) for i, j in up]
        last = lax.slice_in_dim(array, length - width, length, axis=dim)
        leading = lax.slice_in_dim(array, 0, width, axis=dim)
        before = lax.ppermute(last, axis, up)
        after = lax.ppermute(leading, axis, down)
        array = jnp.concatenate([before, array, after], axis=dim)
    return array


def slope(field_value):
    logistic = jax.nn.sigmoid(field_value)
    return logistic * (1.0 + field_value * (1.0 - logistic))


def pad_columns(field_value):
    return jnp.pad(field_value, ((0, 0), (0, 0), (1, 1), (0, 0)))


def shifted(padded, row_offset, col_offset, row_count, rim_start):
    col_count = padded.shape[2] - 2
    return padded[
        :,
        rim_start - row_offset : rim_start - row_offset + row_count,
        1 - col_offset : 1 - col_offset + col_count,
        :,
    ]


def weight_terms(left_field, padded, rim_start):
    row_count = left_field.shape[1]
    tap_list = []
    for row_offset in (-1, 0, 1):
        for col_offset in (-1, 0, 1):
            shifted_piece = shifted(padded, row_offset, col_offset, row_count, rim_start)
            tap_list.append(
                lax.dot_general(
                    left_field,
                    shifted_piece,
                    (((0, 1, 2), (0, 1, 2)), ((), ())),
                    preferred_element_type=jnp.float32,
                )
            )
    stacked = jnp.stack(tap_list)
    return stacked.reshape(-1, stacked.shape[2])


def back_terms(padded, weight, row_count, rim_start):
    accumulated = None
    for row_offset in (-1, 0, 1):
        for col_offset in (-1, 0, 1):
            shifted_piece = shifted(padded, row_offset, col_offset, row_count, rim_start)
            product = lax.dot_general(
                shifted_piece,
                weight[row_offset + 1, col_offset + 1],
                (((3,), (1,)), ((), ())),
                preferred_element_type=jnp.float32,
            )
            accumulated = product if accumulated is None else accumulated + product
    return accumulated


def swap(array, axis, step):
    peers = lax.axis_size(axis)
    return lax.ppermute(array, axis, [(i, i ^ step) for i in range(peers)])


def halve_step(blocks, axis, bit, dim):
    own = (lax.axis_index(axis) >> bit) & 1
    keep = lax.dynamic_index_in_dim(blocks, own, axis=dim, keepdims=False)
    give = lax.dynamic_index_in_dim(blocks, 1 - own, axis=dim, keepdims=False)
    half = give.shape[0] // 2
    if half == 0:
        return keep + swap(give, axis, 1 << bit)
    got = [swap(give[:half], axis, 1 << bit), swap(give[half:], axis, 1 << bit)]
    return keep + jnp.concatenate(got, axis=0)


def settle_stages(grad_scale):
    dates, bands = lax.axis_size("date"), lax.axis_size("band")
    band_bits, date_bits = bands.bit_length() - 1, dates.bit_length() - 1
    stages = []

    def start(grad_term):
        rows, cols = grad_term.shape
        piece = rows // (dates * bands)
        blocks = grad_term.reshape((dates,) + (2,) * band_bits + (piece, cols))
        return halve_step(blocks, "band", 0, 1)

    stages.append((start, True))
    orders = [list(range(1, band_bits)), list(range(band_bits - 1, 0, -1))]

    def split(blocks):
        half = blocks.shape[0] // 2
        return (blocks[:half], blocks[half:])

    if band_bits > 1:
        stages.append((split, False))
    for step in range(band_bits - 1):

        def band_step(parts, step=step):
            moved = []
            for part, order in zip(parts, orders):
                bit = order[step]
                done = order[:step]
                left = [b for b in range(1, band_bits) if b not in done]
                moved.append(halve_step(part, "band", bit, 1 + left.index(bit)))
            return tuple(moved)

        stages.append((band_step, True))
    if band_bits > 1:
        stages.append((lambda parts: jnp.concatenate(parts, axis=0), False))

    def to_dates(blocks):
        return blocks.reshape((2,) * date_bits + blocks.shape[-2:])

    stages.append((to_dates, False))
    for bit in range(date_bits):
        stages.append((lambda blocks, bit=bit: halve_step(blocks, "date", bit, date_bits - 1 - bit), True))
    stages.append((lambda block: block * grad_scale, False))
    if band_bits > 1:

        def gather_far(block):
            mine = lax.axis_index("band") >> 1
            count = 1 << (band_bits - 1)
            got = [block] + [swap(block, "band", m << 1) for m in range(1, count)]
            placed = []
            for spot in range(count):
                owner = int(format(spot, "0%db" % (band_bits - 1))[::-1], 2)
                pick = got[0]
                for m in range(1, count):
                    pick = jnp.where((mine ^ m) == owner, got[m], pick)
                placed.append(pick)
            return jnp.stack(placed, axis=0).reshape((2,) * (band_bits - 1) + block.shape)

        stages.append((gather_far, True))

    def gather_near(block):
        other = swap(block, "band", 1)
        low = (lax.axis_index("band") & 1) == 0
        return jnp.stack([jnp.where(low, block, other), jnp.where(low, other, block)], axis=0)

    stages.append((gather_near, True))
    return stages


class Chain:
    def __init__(self, stages, state):
        self.stages, self.state, self.at = stages, state, 0

    def advance(self, count):
        while count > 0 and self.at < len(self.stages):
            stage, sends = self.stages[self.at]
            self.state = stage(self.state)
            self.at += 1
            count -= int(sends)

    def tie(self, value):
        self.state, value = lax.optimization_barrier((self.state, value))
        return value

    def finish(self, rows, cols):
        self.advance(len(self.stages))
        return self.state.reshape(rows, cols)


def tie_chains(first, second):
    first.state, second.state = lax.optimization_barrier((first.state, second.state))


def body(inputs, preact_one, preact_two, cotangent, weight_one, weight_two):
    row_count = inputs.shape[1]
    grad_scale = 1.0 / (inputs.shape[0] * lax.axis_size("date"))
    act_one = jax.nn.silu(preact_one.astype(jnp.float32)).astype(jnp.bfloat16)
    delta_two = (cotangent.astype(jnp.float32) * slope(preact_two.astype(jnp.float32))).astype(
        jnp.bfloat16
    )
    padded_two = pad_columns(extended(delta_two, (("band", 1),), 1))
    term_two = weight_terms(act_one, padded_two, 1)
    out_rows = term_two.shape[0] // lax.axis_size("date")
    back_one = back_terms(padded_two, weight_two, row_count, 1)
    delta_one = (back_one * slope(preact_one.astype(jnp.float32))).astype(jnp.bfloat16)
    padded_one = pad_columns(extended(delta_one, (("band", 1),), 1))
    term_one = weight_terms(inputs, padded_one, 1)
    input_grad = back_terms(padded_one, weight_one, row_count, 1).astype(jnp.bfloat16)
    band_sends = lax.axis_size("band").bit_length() - 1
    date_sends = lax.axis_size("date").bit_length() - 1
    two = Chain(settle_stages(grad_scale), term_two)
    one = Chain(settle_stages(grad_scale), term_one)
    two.advance(band_sends)
    one.advance(1)
    tie_chains(two, one)
    two.advance(date_sends)
    one.advance(band_sends - 1)
    tie_chains(two, one)
    grad_two = two.finish(out_rows, term_two.shape[1])
    grad_one = one.finish(out_rows, term_one.shape[1])
    return (input_grad, grad_one, grad_two)


def solution(mesh):
    placed = (
        P("date", "band", None, None),
        P("date", "band", None, None),
        P("date", "band", None, None),
        P("date", "band", None, None),
        P(),
        P(),
    )
    return jax.shard_map(
        body,
        mesh=mesh,
        in_specs=placed,
        out_specs=(P("date", "band", None, None), P("date", None), P("date", None)),
        check_vma=False,
    )
```

```python
import jax
import jax.numpy as jnp
from jax import lax
from jax.sharding import PartitionSpec as P


def extended(array, sides, width):
    for axis, dim in sides:
        peers, length = (lax.axis_size(axis), array.shape[dim])
        up = [(i, (i + 1) % peers) for i in range(peers - 1)]
        down = [(j, i) for i, j in up]
        last = lax.slice_in_dim(array, length - width, length, axis=dim)
        leading = lax.slice_in_dim(array, 0, width, axis=dim)
        before = lax.ppermute(last, axis, up)
        after = lax.ppermute(leading, axis, down)
        array = jnp.concatenate([before, array, after], axis=dim)
    return array


def slope(field_value):
    logistic = jax.nn.sigmoid(field_value)
    return logistic * (1.0 + field_value * (1.0 - logistic))


def pad_columns(field_value):
    return jnp.pad(field_value, ((0, 0), (0, 0), (1, 1), (0, 0)))


def shifted(padded, row_offset, col_offset, row_count, rim_start):
    col_count = padded.shape[2] - 2
    return padded[
        :,
        rim_start - row_offset : rim_start - row_offset + row_count,
        1 - col_offset : 1 - col_offset + col_count,
        :,
    ]


def weight_terms(left_field, padded, rim_start):
    row_count = left_field.shape[1]
    tap_list = []
    for row_offset in (-1, 0, 1):
        for col_offset in (-1, 0, 1):
            shifted_piece = shifted(padded, row_offset, col_offset, row_count, rim_start)
            tap_list.append(
                lax.dot_general(
                    left_field,
                    shifted_piece,
                    (((0, 1, 2), (0, 1, 2)), ((), ())),
                    preferred_element_type=jnp.float32,
                )
            )
    stacked = jnp.stack(tap_list)
    return stacked.reshape(-1, stacked.shape[2])


def back_terms(padded, weight, row_count, rim_start):
    accumulated = None
    for row_offset in (-1, 0, 1):
        for col_offset in (-1, 0, 1):
            shifted_piece = shifted(padded, row_offset, col_offset, row_count, rim_start)
            product = lax.dot_general(
                shifted_piece,
                weight[row_offset + 1, col_offset + 1],
                (((3,), (1,)), ((), ())),
                preferred_element_type=jnp.float32,
            )
            accumulated = product if accumulated is None else accumulated + product
    return accumulated


def swap(array, axis, step):
    peers = lax.axis_size(axis)
    return lax.ppermute(array, axis, [(i, i ^ step) for i in range(peers)])


def halve_step(blocks, axis, bit, dim):
    own = (lax.axis_index(axis) >> bit) & 1
    keep = lax.dynamic_index_in_dim(blocks, own, axis=dim, keepdims=False)
    give = lax.dynamic_index_in_dim(blocks, 1 - own, axis=dim, keepdims=False)
    half = give.shape[0] // 2
    if half == 0:
        return keep + swap(give, axis, 1 << bit)
    got = [swap(give[:half], axis, 1 << bit), swap(give[half:], axis, 1 << bit)]
    return keep + jnp.concatenate(got, axis=0)


def settle_stages(grad_scale):
    dates, bands = lax.axis_size("date"), lax.axis_size("band")
    band_bits, date_bits = bands.bit_length() - 1, dates.bit_length() - 1
    stages = []

    def start(grad_term):
        rows, cols = grad_term.shape
        piece = rows // (dates * bands)
        blocks = grad_term.reshape((dates,) + (2,) * band_bits + (piece, cols))
        return halve_step(blocks, "band", 0, 1)

    stages.append((start, True))
    orders = [list(range(1, band_bits)), list(range(band_bits - 1, 0, -1))]

    def split(blocks):
        half = blocks.shape[0] // 2
        return (blocks[:half], blocks[half:])

    if band_bits > 1:
        stages.append((split, False))
    for step in range(band_bits - 1):

        def band_step(parts, step=step):
            moved = []
            for part, order in zip(parts, orders):
                bit = order[step]
                done = order[:step]
                left = [b for b in range(1, band_bits) if b not in done]
                moved.append(halve_step(part, "band", bit, 1 + left.index(bit)))
            return tuple(moved)

        stages.append((band_step, True))
    if band_bits > 1:
        stages.append((lambda parts: jnp.concatenate(parts, axis=0), False))

    def to_dates(blocks):
        return blocks.reshape((2,) * date_bits + blocks.shape[-2:])

    stages.append((to_dates, False))
    def date_direct(blocks):
        blocks = blocks.reshape((dates,) + blocks.shape[date_bits:])
        mine = lax.axis_index("date")
        total = lax.dynamic_index_in_dim(blocks, mine, axis=0, keepdims=False)
        for m in range(1, dates):
            give = lax.dynamic_index_in_dim(blocks, mine ^ m, axis=0, keepdims=False)
            total = total + swap(give, "date", m)
        return total

    stages.append((date_direct, True))
    stages.append((lambda block: block * grad_scale, False))
    if band_bits > 1:

        def gather_far(block):
            mine = lax.axis_index("band") >> 1
            count = 1 << (band_bits - 1)
            got = [block] + [swap(block, "band", m << 1) for m in range(1, count)]
            placed = []
            for spot in range(count):
                owner = int(format(spot, "0%db" % (band_bits - 1))[::-1], 2)
                pick = got[0]
                for m in range(1, count):
                    pick = jnp.where((mine ^ m) == owner, got[m], pick)
                placed.append(pick)
            return jnp.stack(placed, axis=0).reshape((2,) * (band_bits - 1) + block.shape)

        stages.append((gather_far, True))

    def gather_near(block):
        other = swap(block, "band", 1)
        low = (lax.axis_index("band") & 1) == 0
        return jnp.stack([jnp.where(low, block, other), jnp.where(low, other, block)], axis=0)

    stages.append((gather_near, True))
    return stages


class Chain:
    def __init__(self, stages, state):
        self.stages, self.state, self.at = stages, state, 0

    def advance(self, count):
        while count > 0 and self.at < len(self.stages):
            stage, sends = self.stages[self.at]
            self.state = stage(self.state)
            self.at += 1
            count -= int(sends)

    def tie(self, value):
        self.state, value = lax.optimization_barrier((self.state, value))
        return value

    def finish(self, rows, cols):
        self.advance(len(self.stages))
        return self.state.reshape(rows, cols)


def tie_chains(first, second):
    first.state, second.state = lax.optimization_barrier((first.state, second.state))


def body(inputs, preact_one, preact_two, cotangent, weight_one, weight_two):
    row_count = inputs.shape[1]
    grad_scale = 1.0 / (inputs.shape[0] * lax.axis_size("date"))
    act_one = jax.nn.silu(preact_one.astype(jnp.float32)).astype(jnp.bfloat16)
    delta_two = (cotangent.astype(jnp.float32) * slope(preact_two.astype(jnp.float32))).astype(
        jnp.bfloat16
    )
    padded_two = pad_columns(extended(delta_two, (("band", 1),), 1))
    term_two = weight_terms(act_one, padded_two, 1)
    out_rows = term_two.shape[0] // lax.axis_size("date")
    back_one = back_terms(padded_two, weight_two, row_count, 1)
    delta_one = (back_one * slope(preact_one.astype(jnp.float32))).astype(jnp.bfloat16)
    padded_one = pad_columns(extended(delta_one, (("band", 1),), 1))
    term_one = weight_terms(inputs, padded_one, 1)
    input_grad = back_terms(padded_one, weight_one, row_count, 1).astype(jnp.bfloat16)
    band_sends = lax.axis_size("band").bit_length() - 1
    date_sends = 1
    two = Chain(settle_stages(grad_scale), term_two)
    one = Chain(settle_stages(grad_scale), term_one)
    two.advance(band_sends)
    one.advance(1)
    tie_chains(two, one)
    two.advance(date_sends)
    one.advance(band_sends - 1)
    tie_chains(two, one)
    grad_two = two.finish(out_rows, term_two.shape[1])
    grad_one = one.finish(out_rows, term_one.shape[1])
    return (input_grad, grad_one, grad_two)


def solution(mesh):
    placed = (
        P("date", "band", None, None),
        P("date", "band", None, None),
        P("date", "band", None, None),
        P("date", "band", None, None),
        P(),
        P(),
    )
    return jax.shard_map(
        body,
        mesh=mesh,
        in_specs=placed,
        out_specs=(P("date", "band", None, None), P("date", None), P("date", None)),
        check_vma=False,
    )
```

```python
import jax
import jax.numpy as jnp
from jax import lax
from jax.sharding import PartitionSpec as P


def extended(array, sides, width):
    for axis, dim in sides:
        peers, length = (lax.axis_size(axis), array.shape[dim])
        up = [(i, (i + 1) % peers) for i in range(peers - 1)]
        down = [(j, i) for i, j in up]
        last = lax.slice_in_dim(array, length - width, length, axis=dim)
        leading = lax.slice_in_dim(array, 0, width, axis=dim)
        before = lax.ppermute(last, axis, up)
        after = lax.ppermute(leading, axis, down)
        array = jnp.concatenate([before, array, after], axis=dim)
    return array


def slope(field_value):
    logistic = jax.nn.sigmoid(field_value)
    return logistic * (1.0 + field_value * (1.0 - logistic))


def pad_columns(field_value):
    return jnp.pad(field_value, ((0, 0), (0, 0), (1, 1), (0, 0)))


def shifted(padded, row_offset, col_offset, row_count, rim_start):
    col_count = padded.shape[2] - 2
    return padded[
        :,
        rim_start - row_offset : rim_start - row_offset + row_count,
        1 - col_offset : 1 - col_offset + col_count,
        :,
    ]


def weight_terms(left_field, padded, rim_start):
    row_count = left_field.shape[1]
    tap_list = []
    for row_offset in (-1, 0, 1):
        for col_offset in (-1, 0, 1):
            shifted_piece = shifted(padded, row_offset, col_offset, row_count, rim_start)
            tap_list.append(
                lax.dot_general(
                    left_field,
                    shifted_piece,
                    (((0, 1, 2), (0, 1, 2)), ((), ())),
                    preferred_element_type=jnp.float32,
                )
            )
    stacked = jnp.stack(tap_list)
    return stacked.reshape(-1, stacked.shape[2])


def back_terms(padded, weight, row_count, rim_start):
    accumulated = None
    for row_offset in (-1, 0, 1):
        for col_offset in (-1, 0, 1):
            shifted_piece = shifted(padded, row_offset, col_offset, row_count, rim_start)
            product = lax.dot_general(
                shifted_piece,
                weight[row_offset + 1, col_offset + 1],
                (((3,), (1,)), ((), ())),
                preferred_element_type=jnp.float32,
            )
            accumulated = product if accumulated is None else accumulated + product
    return accumulated


def swap(array, axis, step):
    peers = lax.axis_size(axis)
    return lax.ppermute(array, axis, [(i, i ^ step) for i in range(peers)])


def halve_step(blocks, axis, bit, dim):
    own = (lax.axis_index(axis) >> bit) & 1
    keep = lax.dynamic_index_in_dim(blocks, own, axis=dim, keepdims=False)
    give = lax.dynamic_index_in_dim(blocks, 1 - own, axis=dim, keepdims=False)
    half = give.shape[0] // 2
    if half == 0:
        return keep + swap(give, axis, 1 << bit)
    got = [swap(give[:half], axis, 1 << bit), swap(give[half:], axis, 1 << bit)]
    return keep + jnp.concatenate(got, axis=0)


def settle_stages(grad_scale):
    dates, bands = lax.axis_size("date"), lax.axis_size("band")
    band_bits, date_bits = bands.bit_length() - 1, dates.bit_length() - 1
    stages = []

    def start(grad_term):
        rows, cols = grad_term.shape
        piece = rows // (dates * bands)
        blocks = grad_term.reshape((dates,) + (2,) * band_bits + (piece, cols))
        return halve_step(blocks, "band", 0, 1)

    stages.append((start, True))
    orders = [list(range(1, band_bits)), list(range(band_bits - 1, 0, -1))]

    def split(blocks):
        half = blocks.shape[0] // 2
        return (blocks[:half], blocks[half:])

    if band_bits > 1:
        stages.append((split, False))
    for step in range(band_bits - 1):

        def band_step(parts, step=step):
            moved = []
            for part, order in zip(parts, orders):
                bit = order[step]
                done = order[:step]
                left = [b for b in range(1, band_bits) if b not in done]
                moved.append(halve_step(part, "band", bit, 1 + left.index(bit)))
            return tuple(moved)

        stages.append((band_step, True))
    if band_bits > 1:
        stages.append((lambda parts: jnp.concatenate(parts, axis=0), False))

    def to_dates(blocks):
        return blocks.reshape((2,) * date_bits + blocks.shape[-2:])

    stages.append((to_dates, False))
    for bit in range(date_bits):
        stages.append((lambda blocks, bit=bit: halve_step(blocks, "date", bit, date_bits - 1 - bit), True))
    stages.append((lambda block: block * grad_scale, False))
    if band_bits > 1:

        def gather_far(block):
            mine = lax.axis_index("band") >> 1
            count = 1 << (band_bits - 1)
            got = [block] + [swap(block, "band", m << 1) for m in range(1, count)]
            placed = []
            for spot in range(count):
                owner = int(format(spot, "0%db" % (band_bits - 1))[::-1], 2)
                pick = got[0]
                for m in range(1, count):
                    pick = jnp.where((mine ^ m) == owner, got[m], pick)
                placed.append(pick)
            return jnp.stack(placed, axis=0).reshape((2,) * (band_bits - 1) + block.shape)

        stages.append((gather_far, True))

    def gather_near(block):
        other = swap(block, "band", 1)
        low = (lax.axis_index("band") & 1) == 0
        return jnp.stack([jnp.where(low, block, other), jnp.where(low, other, block)], axis=0)

    stages.append((gather_near, True))
    return stages


class Chain:
    def __init__(self, stages, state):
        self.stages, self.state, self.at = stages, state, 0

    def advance(self, count):
        while count > 0 and self.at < len(self.stages):
            stage, sends = self.stages[self.at]
            self.state = stage(self.state)
            self.at += 1
            count -= int(sends)

    def tie(self, value):
        self.state, value = lax.optimization_barrier((self.state, value))
        return value

    def finish(self, rows, cols):
        self.advance(len(self.stages))
        return self.state.reshape(rows, cols)


def tie_chains(first, second):
    first.state, second.state = lax.optimization_barrier((first.state, second.state))


def body(inputs, preact_one, preact_two, cotangent, weight_one, weight_two):
    row_count = inputs.shape[1]
    grad_scale = 1.0 / (inputs.shape[0] * lax.axis_size("date"))
    act_one = jax.nn.silu(preact_one.astype(jnp.float32)).astype(jnp.bfloat16)
    delta_two = (cotangent.astype(jnp.float32) * slope(preact_two.astype(jnp.float32))).astype(
        jnp.bfloat16
    )
    padded_two = pad_columns(extended(delta_two, (("band", 1),), 1))
    term_two = weight_terms(act_one, padded_two, 1)
    out_rows = term_two.shape[0] // lax.axis_size("date")
    back_one = back_terms(padded_two, weight_two, row_count, 1)
    delta_one = (back_one * slope(preact_one.astype(jnp.float32))).astype(jnp.bfloat16)
    padded_one = pad_columns(extended(delta_one, (("band", 1),), 1))
    term_one = weight_terms(inputs, padded_one, 1)
    input_grad = back_terms(padded_one, weight_one, row_count, 1).astype(jnp.bfloat16)
    band_sends = lax.axis_size("band").bit_length() - 1
    date_sends = lax.axis_size("date").bit_length() - 1
    two = Chain(settle_stages(grad_scale), term_two)
    one = Chain(settle_stages(grad_scale), term_one)
    two.advance(band_sends)
    one.advance(1)
    tie_chains(two, one)
    two.advance(date_sends)
    one.advance(band_sends - 1)
    tie_chains(two, one)
    grad_two = two.finish(out_rows, term_two.shape[1])
    one.advance(date_sends)
    one.state, grad_two, input_grad = lax.optimization_barrier((one.state, grad_two, input_grad))
    grad_one = one.finish(out_rows, term_one.shape[1])
    return (input_grad, grad_one, grad_two)


def solution(mesh):
    placed = (
        P("date", "band", None, None),
        P("date", "band", None, None),
        P("date", "band", None, None),
        P("date", "band", None, None),
        P(),
        P(),
    )
    return jax.shard_map(
        body,
        mesh=mesh,
        in_specs=placed,
        out_specs=(P("date", "band", None, None), P("date", None), P("date", None)),
        check_vma=False,
    )
```

```python
import jax
import jax.numpy as jnp
from jax import lax
from jax.sharding import PartitionSpec as P


def extended(array, sides, width):
    for axis, dim in sides:
        peers, length = (lax.axis_size(axis), array.shape[dim])
        up = [(i, (i + 1) % peers) for i in range(peers - 1)]
        down = [(j, i) for i, j in up]
        last = lax.slice_in_dim(array, length - width, length, axis=dim)
        leading = lax.slice_in_dim(array, 0, width, axis=dim)
        before = lax.ppermute(last, axis, up)
        after = lax.ppermute(leading, axis, down)
        array = jnp.concatenate([before, array, after], axis=dim)
    return array


def slope(field_value):
    logistic = jax.nn.sigmoid(field_value)
    return logistic * (1.0 + field_value * (1.0 - logistic))


def pad_columns(field_value):
    return jnp.pad(field_value, ((0, 0), (0, 0), (1, 1), (0, 0)))


def shifted(padded, row_offset, col_offset, row_count, rim_start):
    col_count = padded.shape[2] - 2
    return padded[
        :,
        rim_start - row_offset : rim_start - row_offset + row_count,
        1 - col_offset : 1 - col_offset + col_count,
        :,
    ]


def weight_terms(left_field, padded, rim_start):
    row_count = left_field.shape[1]
    tap_list = []
    for row_offset in (-1, 0, 1):
        for col_offset in (-1, 0, 1):
            shifted_piece = shifted(padded, row_offset, col_offset, row_count, rim_start)
            tap_list.append(
                lax.dot_general(
                    left_field,
                    shifted_piece,
                    (((0, 1, 2), (0, 1, 2)), ((), ())),
                    preferred_element_type=jnp.float32,
                )
            )
    stacked = jnp.stack(tap_list)
    return stacked.reshape(-1, stacked.shape[2])


def back_terms(padded, weight, row_count, rim_start):
    accumulated = None
    for row_offset in (-1, 0, 1):
        for col_offset in (-1, 0, 1):
            shifted_piece = shifted(padded, row_offset, col_offset, row_count, rim_start)
            product = lax.dot_general(
                shifted_piece,
                weight[row_offset + 1, col_offset + 1],
                (((3,), (1,)), ((), ())),
                preferred_element_type=jnp.float32,
            )
            accumulated = product if accumulated is None else accumulated + product
    return accumulated


def swap(array, axis, step):
    peers = lax.axis_size(axis)
    return lax.ppermute(array, axis, [(i, i ^ step) for i in range(peers)])


def halve_step(blocks, axis, bit, dim):
    own = (lax.axis_index(axis) >> bit) & 1
    keep = lax.dynamic_index_in_dim(blocks, own, axis=dim, keepdims=False)
    give = lax.dynamic_index_in_dim(blocks, 1 - own, axis=dim, keepdims=False)
    half = give.shape[0] // 2
    if half == 0:
        return keep + swap(give, axis, 1 << bit)
    got = [swap(give[:half], axis, 1 << bit), swap(give[half:], axis, 1 << bit)]
    return keep + jnp.concatenate(got, axis=0)


def settle_stages(grad_scale):
    dates, bands = lax.axis_size("date"), lax.axis_size("band")
    band_bits, date_bits = bands.bit_length() - 1, dates.bit_length() - 1
    stages = []

    def start(grad_term):
        rows, cols = grad_term.shape
        piece = rows // (dates * bands)
        blocks = grad_term.reshape((dates,) + (2,) * band_bits + (piece, cols))
        return halve_step(blocks, "band", 0, 1)

    stages.append((start, True))
    orders = [list(range(1, band_bits)), list(range(band_bits - 1, 0, -1))]

    def split(blocks):
        half = blocks.shape[0] // 2
        return (blocks[:half], blocks[half:])

    if band_bits > 1:
        stages.append((split, False))
    for step in range(band_bits - 1):

        def band_step(parts, step=step):
            moved = []
            for part, order in zip(parts, orders):
                bit = order[step]
                done = order[:step]
                left = [b for b in range(1, band_bits) if b not in done]
                moved.append(halve_step(part, "band", bit, 1 + left.index(bit)))
            return tuple(moved)

        stages.append((band_step, True))
    if band_bits > 1:
        stages.append((lambda parts: jnp.concatenate(parts, axis=0), False))

    def to_dates(blocks):
        return blocks.reshape((2,) * date_bits + blocks.shape[-2:])

    stages.append((to_dates, False))
    for bit in range(date_bits):
        stages.append((lambda blocks, bit=bit: halve_step(blocks, "date", bit, date_bits - 1 - bit), True))
    stages.append((lambda block: block * grad_scale, False))
    def gather_all(block):
        mine = lax.axis_index("band")
        got = [block] + [swap(block, "band", m) for m in range(1, bands)]
        placed = []
        for spot in range(bands):
            owner = int(format(spot, "0%db" % band_bits)[::-1], 2)
            pick = got[0]
            for m in range(1, bands):
                pick = jnp.where((mine ^ m) == owner, got[m], pick)
            placed.append(pick)
        return jnp.stack(placed, axis=0)

    stages.append((gather_all, True))
    return stages


class Chain:
    def __init__(self, stages, state):
        self.stages, self.state, self.at = stages, state, 0

    def advance(self, count):
        while count > 0 and self.at < len(self.stages):
            stage, sends = self.stages[self.at]
            self.state = stage(self.state)
            self.at += 1
            count -= int(sends)

    def tie(self, value):
        self.state, value = lax.optimization_barrier((self.state, value))
        return value

    def finish(self, rows, cols):
        self.advance(len(self.stages))
        return self.state.reshape(rows, cols)


def tie_chains(first, second):
    first.state, second.state = lax.optimization_barrier((first.state, second.state))


def body(inputs, preact_one, preact_two, cotangent, weight_one, weight_two):
    row_count = inputs.shape[1]
    grad_scale = 1.0 / (inputs.shape[0] * lax.axis_size("date"))
    act_one = jax.nn.silu(preact_one.astype(jnp.float32)).astype(jnp.bfloat16)
    delta_two = (cotangent.astype(jnp.float32) * slope(preact_two.astype(jnp.float32))).astype(
        jnp.bfloat16
    )
    padded_two = pad_columns(extended(delta_two, (("band", 1),), 1))
    term_two = weight_terms(act_one, padded_two, 1)
    out_rows = term_two.shape[0] // lax.axis_size("date")
    back_one = back_terms(padded_two, weight_two, row_count, 1)
    delta_one = (back_one * slope(preact_one.astype(jnp.float32))).astype(jnp.bfloat16)
    padded_one = pad_columns(extended(delta_one, (("band", 1),), 1))
    term_one = weight_terms(inputs, padded_one, 1)
    input_grad = back_terms(padded_one, weight_one, row_count, 1).astype(jnp.bfloat16)
    band_sends = lax.axis_size("band").bit_length() - 1
    date_sends = lax.axis_size("date").bit_length() - 1
    two = Chain(settle_stages(grad_scale), term_two)
    one = Chain(settle_stages(grad_scale), term_one)
    two.advance(band_sends)
    one.advance(1)
    tie_chains(two, one)
    two.advance(date_sends)
    one.advance(band_sends - 1)
    tie_chains(two, one)
    grad_two = two.finish(out_rows, term_two.shape[1])
    grad_one = one.finish(out_rows, term_one.shape[1])
    return (input_grad, grad_one, grad_two)


def solution(mesh):
    placed = (
        P("date", "band", None, None),
        P("date", "band", None, None),
        P("date", "band", None, None),
        P("date", "band", None, None),
        P(),
        P(),
    )
    return jax.shard_map(
        body,
        mesh=mesh,
        in_specs=placed,
        out_specs=(P("date", "band", None, None), P("date", None), P("date", None)),
        check_vma=False,
    )
```

```python
import jax
import jax.numpy as jnp
from jax import lax
from jax.sharding import PartitionSpec as P


def extended(array, sides, width):
    for axis, dim in sides:
        peers, length = (lax.axis_size(axis), array.shape[dim])
        up = [(i, (i + 1) % peers) for i in range(peers - 1)]
        down = [(j, i) for i, j in up]
        last = lax.slice_in_dim(array, length - width, length, axis=dim)
        leading = lax.slice_in_dim(array, 0, width, axis=dim)
        before = lax.ppermute(last, axis, up)
        after = lax.ppermute(leading, axis, down)
        array = jnp.concatenate([before, array, after], axis=dim)
    return array


def slope(field_value):
    logistic = jax.nn.sigmoid(field_value)
    return logistic * (1.0 + field_value * (1.0 - logistic))


def pad_columns(field_value):
    return jnp.pad(field_value, ((0, 0), (0, 0), (1, 1), (0, 0)))


def shifted(padded, row_offset, col_offset, row_count, rim_start):
    col_count = padded.shape[2] - 2
    return padded[
        :,
        rim_start - row_offset : rim_start - row_offset + row_count,
        1 - col_offset : 1 - col_offset + col_count,
        :,
    ]


def weight_terms(left_field, padded, rim_start):
    row_count = left_field.shape[1]
    tap_list = []
    for row_offset in (-1, 0, 1):
        for col_offset in (-1, 0, 1):
            shifted_piece = shifted(padded, row_offset, col_offset, row_count, rim_start)
            tap_list.append(
                lax.dot_general(
                    left_field,
                    shifted_piece,
                    (((0, 1, 2), (0, 1, 2)), ((), ())),
                    preferred_element_type=jnp.float32,
                )
            )
    stacked = jnp.stack(tap_list)
    return stacked.reshape(-1, stacked.shape[2])


def back_terms(padded, weight, row_count, rim_start):
    accumulated = None
    for row_offset in (-1, 0, 1):
        for col_offset in (-1, 0, 1):
            shifted_piece = shifted(padded, row_offset, col_offset, row_count, rim_start)
            product = lax.dot_general(
                shifted_piece,
                weight[row_offset + 1, col_offset + 1],
                (((3,), (1,)), ((), ())),
                preferred_element_type=jnp.float32,
            )
            accumulated = product if accumulated is None else accumulated + product
    return accumulated


def swap(array, axis, step):
    peers = lax.axis_size(axis)
    return lax.ppermute(array, axis, [(i, i ^ step) for i in range(peers)])


def halve_step(blocks, axis, bit, dim):
    own = (lax.axis_index(axis) >> bit) & 1
    keep = lax.dynamic_index_in_dim(blocks, own, axis=dim, keepdims=False)
    give = lax.dynamic_index_in_dim(blocks, 1 - own, axis=dim, keepdims=False)
    half = give.shape[0] // 2
    if half == 0:
        return keep + swap(give, axis, 1 << bit)
    got = [swap(give[:half], axis, 1 << bit), swap(give[half:], axis, 1 << bit)]
    return keep + jnp.concatenate(got, axis=0)


def settle_stages(grad_scale):
    dates, bands = lax.axis_size("date"), lax.axis_size("band")
    band_bits, date_bits = bands.bit_length() - 1, dates.bit_length() - 1
    stages = []

    def start(grad_term):
        rows, cols = grad_term.shape
        piece = rows // (dates * bands)
        blocks = grad_term.reshape((dates,) + (2,) * band_bits + (piece, cols))
        return halve_step(blocks, "band", 0, 1)

    stages.append((start, True))
    orders = [list(range(1, band_bits)), list(range(band_bits - 1, 0, -1))]

    def split(blocks):
        half = blocks.shape[0] // 2
        return (blocks[:half], blocks[half:])

    if band_bits > 1:
        stages.append((split, False))
    for step in range(band_bits - 1):

        def band_step(parts, step=step):
            moved = []
            for part, order in zip(parts, orders):
                bit = order[step]
                done = order[:step]
                left = [b for b in range(1, band_bits) if b not in done]
                moved.append(halve_step(part, "band", bit, 1 + left.index(bit)))
            return tuple(moved)

        stages.append((band_step, True))
    if band_bits > 1:
        stages.append((lambda parts: jnp.concatenate(parts, axis=0), False))

    def to_dates(blocks):
        return blocks.reshape((2,) * date_bits + blocks.shape[-2:])

    stages.append((to_dates, False))
    for bit in range(date_bits):
        stages.append((lambda blocks, bit=bit: halve_step(blocks, "date", bit, date_bits - 1 - bit), True))
    stages.append((lambda block: block * grad_scale, False))
    if band_bits > 1:

        def gather_far(block):
            mine = lax.axis_index("band") >> 1
            count = 1 << (band_bits - 1)
            got = [block] + [swap(block, "band", m << 1) for m in range(1, count)]
            placed = []
            for spot in range(count):
                owner = int(format(spot, "0%db" % (band_bits - 1))[::-1], 2)
                pick = got[0]
                for m in range(1, count):
                    pick = jnp.where((mine ^ m) == owner, got[m], pick)
                placed.append(pick)
            return jnp.stack(placed, axis=0).reshape((2,) * (band_bits - 1) + block.shape)

        stages.append((gather_far, True))

    def gather_near(block):
        other = swap(block, "band", 1)
        low = (lax.axis_index("band") & 1) == 0
        return jnp.stack([jnp.where(low, block, other), jnp.where(low, other, block)], axis=0)

    stages.append((gather_near, True))
    return stages


class Chain:
    def __init__(self, stages, state):
        self.stages, self.state, self.at = stages, state, 0

    def advance(self, count):
        while count > 0 and self.at < len(self.stages):
            stage, sends = self.stages[self.at]
            self.state = stage(self.state)
            self.at += 1
            count -= int(sends)

    def tie(self, value):
        self.state, value = lax.optimization_barrier((self.state, value))
        return value

    def finish(self, rows, cols):
        self.advance(len(self.stages))
        return self.state.reshape(rows, cols)


def tie_chains(first, second):
    first.state, second.state = lax.optimization_barrier((first.state, second.state))


def body(inputs, preact_one, preact_two, cotangent, weight_one, weight_two):
    row_count = inputs.shape[1]
    grad_scale = 1.0 / (inputs.shape[0] * lax.axis_size("date"))
    act_one = jax.nn.silu(preact_one.astype(jnp.float32)).astype(jnp.bfloat16)
    delta_two = (cotangent.astype(jnp.float32) * slope(preact_two.astype(jnp.float32))).astype(
        jnp.bfloat16
    )
    padded_two = pad_columns(extended(delta_two, (("band", 1),), 1))
    term_two = weight_terms(act_one, padded_two, 1)
    out_rows = term_two.shape[0] // lax.axis_size("date")
    back_one = back_terms(padded_two, weight_two, row_count, 1)
    delta_one = (back_one * slope(preact_one.astype(jnp.float32))).astype(jnp.bfloat16)
    padded_one = pad_columns(extended(delta_one, (("band", 1),), 1))
    term_one = weight_terms(inputs, padded_one, 1)
    input_grad = back_terms(padded_one, weight_one, row_count, 1).astype(jnp.bfloat16)
    band_sends = lax.axis_size("band").bit_length() - 1
    date_sends = lax.axis_size("date").bit_length() - 1
    two = Chain(settle_stages(grad_scale), term_two)
    one = Chain(settle_stages(grad_scale), term_one)
    two.advance(band_sends)
    one.advance(1)
    tie_chains(two, one)
    two.advance(date_sends)
    one.advance(band_sends - 1)
    tie_chains(two, one)
    grad_two = two.finish(out_rows, term_two.shape[1])
    one.advance(date_sends)
    one.state, input_grad = lax.optimization_barrier((one.state, input_grad))
    grad_one = one.finish(out_rows, term_one.shape[1])
    return (input_grad, grad_one, grad_two)


def solution(mesh):
    placed = (
        P("date", "band", None, None),
        P("date", "band", None, None),
        P("date", "band", None, None),
        P("date", "band", None, None),
        P(),
        P(),
    )
    return jax.shard_map(
        body,
        mesh=mesh,
        in_specs=placed,
        out_specs=(P("date", "band", None, None), P("date", None), P("date", None)),
        check_vma=False,
    )
```

```python
import jax
import jax.numpy as jnp
from jax import lax
from jax.sharding import PartitionSpec as P


def extended(array, sides, width):
    for axis, dim in sides:
        peers, length = (lax.axis_size(axis), array.shape[dim])
        up = [(i, (i + 1) % peers) for i in range(peers - 1)]
        down = [(j, i) for i, j in up]
        last = lax.slice_in_dim(array, length - width, length, axis=dim)
        leading = lax.slice_in_dim(array, 0, width, axis=dim)
        before = lax.ppermute(last, axis, up)
        after = lax.ppermute(leading, axis, down)
        array = jnp.concatenate([before, array, after], axis=dim)
    return array


def slope(field_value):
    logistic = jax.nn.sigmoid(field_value)
    return logistic * (1.0 + field_value * (1.0 - logistic))


def pad_columns(field_value):
    return jnp.pad(field_value, ((0, 0), (0, 0), (1, 1), (0, 0)))


def shifted(padded, row_offset, col_offset, row_count, rim_start):
    col_count = padded.shape[2] - 2
    return padded[
        :,
        rim_start - row_offset : rim_start - row_offset + row_count,
        1 - col_offset : 1 - col_offset + col_count,
        :,
    ]


def weight_terms(left_field, padded, rim_start):
    row_count = left_field.shape[1]
    tap_list = []
    for row_offset in (-1, 0, 1):
        for col_offset in (-1, 0, 1):
            shifted_piece = shifted(padded, row_offset, col_offset, row_count, rim_start)
            tap_list.append(
                lax.dot_general(
                    left_field,
                    shifted_piece,
                    (((0, 1, 2), (0, 1, 2)), ((), ())),
                    preferred_element_type=jnp.float32,
                )
            )
    stacked = jnp.stack(tap_list)
    return stacked.reshape(-1, stacked.shape[2])


def back_terms(padded, weight, row_count, rim_start):
    accumulated = None
    for row_offset in (-1, 0, 1):
        for col_offset in (-1, 0, 1):
            shifted_piece = shifted(padded, row_offset, col_offset, row_count, rim_start)
            product = lax.dot_general(
                shifted_piece,
                weight[row_offset + 1, col_offset + 1],
                (((3,), (1,)), ((), ())),
                preferred_element_type=jnp.float32,
            )
            accumulated = product if accumulated is None else accumulated + product
    return accumulated


def swap(array, axis, step):
    peers = lax.axis_size(axis)
    return lax.ppermute(array, axis, [(i, i ^ step) for i in range(peers)])


def halve_step(blocks, axis, bit, dim):
    own = (lax.axis_index(axis) >> bit) & 1
    keep = lax.dynamic_index_in_dim(blocks, own, axis=dim, keepdims=False)
    give = lax.dynamic_index_in_dim(blocks, 1 - own, axis=dim, keepdims=False)
    half = give.shape[0] // 2
    if half == 0 or (axis == "band" and bit == 0):
        return keep + swap(give, axis, 1 << bit)
    got = [swap(give[:half], axis, 1 << bit), swap(give[half:], axis, 1 << bit)]
    return keep + jnp.concatenate(got, axis=0)


def settle_stages(grad_scale):
    dates, bands = lax.axis_size("date"), lax.axis_size("band")
    band_bits, date_bits = bands.bit_length() - 1, dates.bit_length() - 1
    stages = []

    def start(grad_term):
        rows, cols = grad_term.shape
        piece = rows // (dates * bands)
        blocks = grad_term.reshape((dates,) + (2,) * band_bits + (piece, cols))
        return halve_step(blocks, "band", 0, 1)

    stages.append((start, True))
    orders = [list(range(1, band_bits)), list(range(band_bits - 1, 0, -1))]

    def split(blocks):
        half = blocks.shape[0] // 2
        return (blocks[:half], blocks[half:])

    if band_bits > 1:
        stages.append((split, False))
    for step in range(band_bits - 1):

        def band_step(parts, step=step):
            moved = []
            for part, order in zip(parts, orders):
                bit = order[step]
                done = order[:step]
                left = [b for b in range(1, band_bits) if b not in done]
                moved.append(halve_step(part, "band", bit, 1 + left.index(bit)))
            return tuple(moved)

        stages.append((band_step, True))
    if band_bits > 1:
        stages.append((lambda parts: jnp.concatenate(parts, axis=0), False))

    def to_dates(blocks):
        return blocks.reshape((2,) * date_bits + blocks.shape[-2:])

    stages.append((to_dates, False))
    for bit in range(date_bits):
        stages.append((lambda blocks, bit=bit: halve_step(blocks, "date", bit, date_bits - 1 - bit), True))
    stages.append((lambda block: block * grad_scale, False))
    if band_bits > 1:

        def gather_far(block):
            mine = lax.axis_index("band") >> 1
            count = 1 << (band_bits - 1)
            got = [block] + [swap(block, "band", m << 1) for m in range(1, count)]
            placed = []
            for spot in range(count):
                owner = int(format(spot, "0%db" % (band_bits - 1))[::-1], 2)
                pick = got[0]
                for m in range(1, count):
                    pick = jnp.where((mine ^ m) == owner, got[m], pick)
                placed.append(pick)
            return jnp.stack(placed, axis=0).reshape((2,) * (band_bits - 1) + block.shape)

        stages.append((gather_far, True))

    def gather_near(block):
        other = swap(block, "band", 1)
        low = (lax.axis_index("band") & 1) == 0
        return jnp.stack([jnp.where(low, block, other), jnp.where(low, other, block)], axis=0)

    stages.append((gather_near, True))
    return stages


class Chain:
    def __init__(self, stages, state):
        self.stages, self.state, self.at = stages, state, 0

    def advance(self, count):
        while count > 0 and self.at < len(self.stages):
            stage, sends = self.stages[self.at]
            self.state = stage(self.state)
            self.at += 1
            count -= int(sends)

    def tie(self, value):
        self.state, value = lax.optimization_barrier((self.state, value))
        return value

    def finish(self, rows, cols):
        self.advance(len(self.stages))
        return self.state.reshape(rows, cols)


def tie_chains(first, second):
    first.state, second.state = lax.optimization_barrier((first.state, second.state))


def body(inputs, preact_one, preact_two, cotangent, weight_one, weight_two):
    row_count = inputs.shape[1]
    grad_scale = 1.0 / (inputs.shape[0] * lax.axis_size("date"))
    act_one = jax.nn.silu(preact_one.astype(jnp.float32)).astype(jnp.bfloat16)
    delta_two = (cotangent.astype(jnp.float32) * slope(preact_two.astype(jnp.float32))).astype(
        jnp.bfloat16
    )
    padded_two = pad_columns(extended(delta_two, (("band", 1),), 1))
    term_two = weight_terms(act_one, padded_two, 1)
    out_rows = term_two.shape[0] // lax.axis_size("date")
    back_one = back_terms(padded_two, weight_two, row_count, 1)
    delta_one = (back_one * slope(preact_one.astype(jnp.float32))).astype(jnp.bfloat16)
    padded_one = pad_columns(extended(delta_one, (("band", 1),), 1))
    term_one = weight_terms(inputs, padded_one, 1)
    input_grad = back_terms(padded_one, weight_one, row_count, 1).astype(jnp.bfloat16)
    band_sends = lax.axis_size("band").bit_length() - 1
    date_sends = lax.axis_size("date").bit_length() - 1
    two = Chain(settle_stages(grad_scale), term_two)
    one = Chain(settle_stages(grad_scale), term_one)
    two.advance(band_sends)
    one.advance(1)
    tie_chains(two, one)
    two.advance(date_sends)
    one.advance(band_sends - 1)
    tie_chains(two, one)
    grad_two = two.finish(out_rows, term_two.shape[1])
    grad_one = one.finish(out_rows, term_one.shape[1])
    return (input_grad, grad_one, grad_two)


def solution(mesh):
    placed = (
        P("date", "band", None, None),
        P("date", "band", None, None),
        P("date", "band", None, None),
        P("date", "band", None, None),
        P(),
        P(),
    )
    return jax.shard_map(
        body,
        mesh=mesh,
        in_specs=placed,
        out_specs=(P("date", "band", None, None), P("date", None), P("date", None)),
        check_vma=False,
    )
```

```python
import jax
import jax.numpy as jnp
from jax import lax
from jax.sharding import PartitionSpec as P


def extended(array, sides, width):
    for axis, dim in sides:
        peers, length = (lax.axis_size(axis), array.shape[dim])
        up = [(i, (i + 1) % peers) for i in range(peers - 1)]
        down = [(j, i) for i, j in up]
        last = lax.slice_in_dim(array, length - width, length, axis=dim)
        leading = lax.slice_in_dim(array, 0, width, axis=dim)
        before = lax.ppermute(last, axis, up)
        after = lax.ppermute(leading, axis, down)
        array = jnp.concatenate([before, array, after], axis=dim)
    return array


def slope(field_value):
    logistic = jax.nn.sigmoid(field_value)
    return logistic * (1.0 + field_value * (1.0 - logistic))


def pad_columns(field_value):
    return jnp.pad(field_value, ((0, 0), (0, 0), (1, 1), (0, 0)))


def shifted(padded, row_offset, col_offset, row_count, rim_start):
    col_count = padded.shape[2] - 2
    return padded[
        :,
        rim_start - row_offset : rim_start - row_offset + row_count,
        1 - col_offset : 1 - col_offset + col_count,
        :,
    ]


def weight_terms(left_field, padded, rim_start):
    row_count = left_field.shape[1]
    tap_list = []
    for row_offset in (-1, 0, 1):
        for col_offset in (-1, 0, 1):
            shifted_piece = shifted(padded, row_offset, col_offset, row_count, rim_start)
            tap_list.append(
                lax.dot_general(
                    left_field,
                    shifted_piece,
                    (((0, 1, 2), (0, 1, 2)), ((), ())),
                    preferred_element_type=jnp.float32,
                )
            )
    stacked = jnp.stack(tap_list)
    return stacked.reshape(-1, stacked.shape[2])


def back_terms(padded, weight, row_count, rim_start):
    accumulated = None
    for row_offset in (-1, 0, 1):
        for col_offset in (-1, 0, 1):
            shifted_piece = shifted(padded, row_offset, col_offset, row_count, rim_start)
            product = lax.dot_general(
                shifted_piece,
                weight[row_offset + 1, col_offset + 1],
                (((3,), (1,)), ((), ())),
                preferred_element_type=jnp.float32,
            )
            accumulated = product if accumulated is None else accumulated + product
    return accumulated


def swap(array, axis, step):
    peers = lax.axis_size(axis)
    return lax.ppermute(array, axis, [(i, i ^ step) for i in range(peers)])


def halve_step(blocks, axis, bit, dim):
    own = (lax.axis_index(axis) >> bit) & 1
    keep = lax.dynamic_index_in_dim(blocks, own, axis=dim, keepdims=False)
    give = lax.dynamic_index_in_dim(blocks, 1 - own, axis=dim, keepdims=False)
    half = give.shape[0] // 2
    if half == 0:
        return keep + swap(give, axis, 1 << bit)
    got = [swap(give[:half], axis, 1 << bit), swap(give[half:], axis, 1 << bit)]
    return keep + jnp.concatenate(got, axis=0)


def settle_stages(grad_scale):
    dates, bands = lax.axis_size("date"), lax.axis_size("band")
    band_bits, date_bits = bands.bit_length() - 1, dates.bit_length() - 1
    stages = []

    def start(grad_term):
        rows, cols = grad_term.shape
        piece = rows // (dates * bands)
        blocks = grad_term.reshape((dates,) + (2,) * band_bits + (piece, cols))
        return halve_step(blocks, "band", 0, 1)

    stages.append((start, True))
    orders = [list(range(1, band_bits)), list(range(band_bits - 1, 0, -1))]

    def split(blocks):
        half = blocks.shape[0] // 2
        return (blocks[:half], blocks[half:])

    if band_bits > 1:
        stages.append((split, False))
    for step in range(band_bits - 1):

        def band_step(parts, step=step):
            moved = []
            for part, order in zip(parts, orders):
                bit = order[step]
                done = order[:step]
                left = [b for b in range(1, band_bits) if b not in done]
                moved.append(halve_step(part, "band", bit, 1 + left.index(bit)))
            return tuple(moved)

        stages.append((band_step, True))
    if band_bits > 1:
        stages.append((lambda parts: jnp.concatenate(parts, axis=0), False))

    def to_dates(blocks):
        return blocks.reshape((2,) * date_bits + blocks.shape[-2:])

    stages.append((to_dates, False))
    for bit in range(date_bits):
        stages.append((lambda blocks, bit=bit: halve_step(blocks, "date", bit, date_bits - 1 - bit), True))
    stages.append((lambda block: block * grad_scale, False))
    if band_bits > 1:

        def gather_far(block):
            mine = lax.axis_index("band") >> 1
            count = 1 << (band_bits - 1)
            got = [block] + [swap(block, "band", m << 1) for m in range(1, count)]
            placed = []
            for spot in range(count):
                owner = int(format(spot, "0%db" % (band_bits - 1))[::-1], 2)
                pick = got[0]
                for m in range(1, count):
                    pick = jnp.where((mine ^ m) == owner, got[m], pick)
                placed.append(pick)
            return jnp.stack(placed, axis=0).reshape((2,) * (band_bits - 1) + block.shape)

        stages.append((gather_far, True))

    def gather_near(block):
        other = swap(block, "band", 1)
        low = (lax.axis_index("band") & 1) == 0
        return jnp.stack([jnp.where(low, block, other), jnp.where(low, other, block)], axis=0)

    stages.append((gather_near, True))
    return stages


class Chain:
    def __init__(self, stages, state):
        self.stages, self.state, self.at = stages, state, 0

    def advance(self, count):
        while count > 0 and self.at < len(self.stages):
            stage, sends = self.stages[self.at]
            self.state = stage(self.state)
            self.at += 1
            count -= int(sends)

    def tie(self, value):
        self.state, value = lax.optimization_barrier((self.state, value))
        return value

    def finish(self, rows, cols):
        self.advance(len(self.stages))
        return self.state.reshape(rows, cols)


def tie_chains(first, second):
    first.state, second.state = lax.optimization_barrier((first.state, second.state))


def body(inputs, preact_one, preact_two, cotangent, weight_one, weight_two):
    row_count = inputs.shape[1]
    grad_scale = 1.0 / (inputs.shape[0] * lax.axis_size("date"))
    act_one = jax.nn.silu(preact_one.astype(jnp.float32)).astype(jnp.bfloat16)
    delta_two = (cotangent.astype(jnp.float32) * slope(preact_two.astype(jnp.float32))).astype(
        jnp.bfloat16
    )
    padded_two = pad_columns(extended(delta_two, (("band", 1),), 1))
    term_two = weight_terms(act_one, padded_two, 1)
    out_rows = term_two.shape[0] // lax.axis_size("date")
    back_one = back_terms(padded_two, weight_two, row_count, 1)
    delta_one = (back_one * slope(preact_one.astype(jnp.float32))).astype(jnp.bfloat16)
    padded_one = pad_columns(extended(delta_one, (("band", 1),), 1))
    term_one = weight_terms(inputs, padded_one, 1)
    input_grad = back_terms(padded_one, weight_one, row_count, 1).astype(jnp.bfloat16)
    band_sends = lax.axis_size("band").bit_length() - 1
    date_sends = lax.axis_size("date").bit_length() - 1
    two = Chain(settle_stages(grad_scale), term_two)
    one = Chain(settle_stages(grad_scale), term_one)
    two.advance(band_sends)
    one.advance(1)
    two.advance(date_sends)
    one.advance(band_sends - 1)
    tie_chains(two, one)
    grad_two = two.finish(out_rows, term_two.shape[1])
    grad_one = one.finish(out_rows, term_one.shape[1])
    return (input_grad, grad_one, grad_two)


def solution(mesh):
    placed = (
        P("date", "band", None, None),
        P("date", "band", None, None),
        P("date", "band", None, None),
        P("date", "band", None, None),
        P(),
        P(),
    )
    return jax.shard_map(
        body,
        mesh=mesh,
        in_specs=placed,
        out_specs=(P("date", "band", None, None), P("date", None), P("date", None)),
        check_vma=False,
    )
```

```python
import jax
import jax.numpy as jnp
from jax import lax
from jax.sharding import PartitionSpec as P


def extended(array, sides, width):
    for axis, dim in sides:
        peers, length = (lax.axis_size(axis), array.shape[dim])
        up = [(i, (i + 1) % peers) for i in range(peers - 1)]
        down = [(j, i) for i, j in up]
        last = lax.slice_in_dim(array, length - width, length, axis=dim)
        leading = lax.slice_in_dim(array, 0, width, axis=dim)
        before = lax.ppermute(last, axis, up)
        after = lax.ppermute(leading, axis, down)
        array = jnp.concatenate([before, array, after], axis=dim)
    return array


def slope(field_value):
    logistic = jax.nn.sigmoid(field_value)
    return logistic * (1.0 + field_value * (1.0 - logistic))


def pad_columns(field_value):
    return jnp.pad(field_value, ((0, 0), (0, 0), (1, 1), (0, 0)))


def shifted(padded, row_offset, col_offset, row_count, rim_start):
    col_count = padded.shape[2] - 2
    return padded[
        :,
        rim_start - row_offset : rim_start - row_offset + row_count,
        1 - col_offset : 1 - col_offset + col_count,
        :,
    ]


def weight_terms(left_field, padded, rim_start):
    row_count = left_field.shape[1]
    tap_list = []
    for row_offset in (-1, 0, 1):
        for col_offset in (-1, 0, 1):
            shifted_piece = shifted(padded, row_offset, col_offset, row_count, rim_start)
            tap_list.append(
                lax.dot_general(
                    left_field,
                    shifted_piece,
                    (((0, 1, 2), (0, 1, 2)), ((), ())),
                    preferred_element_type=jnp.float32,
                )
            )
    stacked = jnp.stack(tap_list)
    return stacked.reshape(-1, stacked.shape[2])


def back_terms(padded, weight, row_count, rim_start):
    accumulated = None
    for row_offset in (-1, 0, 1):
        for col_offset in (-1, 0, 1):
            shifted_piece = shifted(padded, row_offset, col_offset, row_count, rim_start)
            product = lax.dot_general(
                shifted_piece,
                weight[row_offset + 1, col_offset + 1],
                (((3,), (1,)), ((), ())),
                preferred_element_type=jnp.float32,
            )
            accumulated = product if accumulated is None else accumulated + product
    return accumulated


def swap(array, axis, step):
    peers = lax.axis_size(axis)
    return lax.ppermute(array, axis, [(i, i ^ step) for i in range(peers)])


def halve_step(blocks, axis, bit, dim):
    own = (lax.axis_index(axis) >> bit) & 1
    keep = lax.dynamic_index_in_dim(blocks, own, axis=dim, keepdims=False)
    give = lax.dynamic_index_in_dim(blocks, 1 - own, axis=dim, keepdims=False)
    half = give.shape[0] // 2
    if half == 0:
        return keep + swap(give, axis, 1 << bit)
    got = [swap(give[:half], axis, 1 << bit), swap(give[half:], axis, 1 << bit)]
    return keep + jnp.concatenate(got, axis=0)


def settle_stages(grad_scale):
    dates, bands = lax.axis_size("date"), lax.axis_size("band")
    band_bits, date_bits = bands.bit_length() - 1, dates.bit_length() - 1
    stages = []

    def start(grad_term):
        rows, cols = grad_term.shape
        piece = rows // (dates * bands)
        blocks = grad_term.reshape((dates,) + (2,) * band_bits + (piece, cols))
        return halve_step(blocks, "band", 0, 1)

    stages.append((start, True))
    orders = [list(range(1, band_bits)), list(range(band_bits - 1, 0, -1))]

    def split(blocks):
        half = blocks.shape[0] // 2
        return (blocks[:half], blocks[half:])

    if band_bits > 1:
        stages.append((split, False))
    for step in range(band_bits - 1):

        def band_step(parts, step=step):
            moved = []
            for part, order in zip(parts, orders):
                bit = order[step]
                done = order[:step]
                left = [b for b in range(1, band_bits) if b not in done]
                moved.append(halve_step(part, "band", bit, 1 + left.index(bit)))
            return tuple(moved)

        stages.append((band_step, True))
    def to_dates(parts):
        return tuple(p.reshape((2,) * (date_bits - 1) + p.shape[-2:]) for p in parts)

    stages.append((to_dates, False))
    for bit in range(date_bits - 1):

        def low_step(parts, bit=bit):
            return tuple(halve_step(p, "date", bit, date_bits - 2 - bit) for p in parts)

        stages.append((low_step, True))

    def top_step(parts):
        blocks = jnp.stack(parts, axis=0)
        return halve_step(blocks, "date", date_bits - 1, 0)

    stages.append((top_step, True))
    stages.append((lambda block: block * grad_scale, False))
    if band_bits > 1:

        def gather_far(block):
            mine = lax.axis_index("band") >> 1
            count = 1 << (band_bits - 1)
            got = [block] + [swap(block, "band", m << 1) for m in range(1, count)]
            placed = []
            for spot in range(count):
                owner = int(format(spot, "0%db" % (band_bits - 1))[::-1], 2)
                pick = got[0]
                for m in range(1, count):
                    pick = jnp.where((mine ^ m) == owner, got[m], pick)
                placed.append(pick)
            return jnp.stack(placed, axis=0).reshape((2,) * (band_bits - 1) + block.shape)

        stages.append((gather_far, True))

    def gather_near(block):
        other = swap(block, "band", 1)
        low = (lax.axis_index("band") & 1) == 0
        return jnp.stack([jnp.where(low, block, other), jnp.where(low, other, block)], axis=0)

    stages.append((gather_near, True))
    return stages


class Chain:
    def __init__(self, stages, state):
        self.stages, self.state, self.at = stages, state, 0

    def advance(self, count):
        while count > 0 and self.at < len(self.stages):
            stage, sends = self.stages[self.at]
            self.state = stage(self.state)
            self.at += 1
            count -= int(sends)

    def tie(self, value):
        self.state, value = lax.optimization_barrier((self.state, value))
        return value

    def finish(self, rows, cols):
        self.advance(len(self.stages))
        return self.state.reshape(rows, cols)


def tie_chains(first, second):
    first.state, second.state = lax.optimization_barrier((first.state, second.state))


def body(inputs, preact_one, preact_two, cotangent, weight_one, weight_two):
    row_count = inputs.shape[1]
    grad_scale = 1.0 / (inputs.shape[0] * lax.axis_size("date"))
    act_one = jax.nn.silu(preact_one.astype(jnp.float32)).astype(jnp.bfloat16)
    delta_two = (cotangent.astype(jnp.float32) * slope(preact_two.astype(jnp.float32))).astype(
        jnp.bfloat16
    )
    padded_two = pad_columns(extended(delta_two, (("band", 1),), 1))
    term_two = weight_terms(act_one, padded_two, 1)
    out_rows = term_two.shape[0] // lax.axis_size("date")
    back_one = back_terms(padded_two, weight_two, row_count, 1)
    delta_one = (back_one * slope(preact_one.astype(jnp.float32))).astype(jnp.bfloat16)
    padded_one = pad_columns(extended(delta_one, (("band", 1),), 1))
    term_one = weight_terms(inputs, padded_one, 1)
    input_grad = back_terms(padded_one, weight_one, row_count, 1).astype(jnp.bfloat16)
    band_sends = lax.axis_size("band").bit_length() - 1
    date_sends = lax.axis_size("date").bit_length() - 1
    two = Chain(settle_stages(grad_scale), term_two)
    one = Chain(settle_stages(grad_scale), term_one)
    two.advance(band_sends)
    one.advance(1)
    tie_chains(two, one)
    two.advance(date_sends)
    one.advance(band_sends - 1)
    tie_chains(two, one)
    grad_two = two.finish(out_rows, term_two.shape[1])
    grad_one = one.finish(out_rows, term_one.shape[1])
    return (input_grad, grad_one, grad_two)


def solution(mesh):
    placed = (
        P("date", "band", None, None),
        P("date", "band", None, None),
        P("date", "band", None, None),
        P("date", "band", None, None),
        P(),
        P(),
    )
    return jax.shard_map(
        body,
        mesh=mesh,
        in_specs=placed,
        out_specs=(P("date", "band", None, None), P("date", None), P("date", None)),
        check_vma=False,
    )
```

```python
import jax
import jax.numpy as jnp
from jax import lax
from jax.sharding import PartitionSpec as P


def extended(array, sides, width):
    for axis, dim in sides:
        peers, length = (lax.axis_size(axis), array.shape[dim])
        up = [(i, (i + 1) % peers) for i in range(peers - 1)]
        down = [(j, i) for i, j in up]
        last = lax.slice_in_dim(array, length - width, length, axis=dim)
        leading = lax.slice_in_dim(array, 0, width, axis=dim)
        before = lax.ppermute(last, axis, up)
        after = lax.ppermute(leading, axis, down)
        array = jnp.concatenate([before, array, after], axis=dim)
    return array


def slope(field_value):
    logistic = jax.nn.sigmoid(field_value)
    return logistic * (1.0 + field_value * (1.0 - logistic))


def pad_columns(field_value):
    return jnp.pad(field_value, ((0, 0), (0, 0), (1, 1), (0, 0)))


def shifted(padded, row_offset, col_offset, row_count, rim_start):
    col_count = padded.shape[2] - 2
    return padded[
        :,
        rim_start - row_offset : rim_start - row_offset + row_count,
        1 - col_offset : 1 - col_offset + col_count,
        :,
    ]


def weight_terms(left_field, padded, rim_start):
    row_count = left_field.shape[1]
    tap_list = []
    for row_offset in (-1, 0, 1):
        for col_offset in (-1, 0, 1):
            shifted_piece = shifted(padded, row_offset, col_offset, row_count, rim_start)
            tap_list.append(
                lax.dot_general(
                    left_field,
                    shifted_piece,
                    (((0, 1, 2), (0, 1, 2)), ((), ())),
                    preferred_element_type=jnp.float32,
                )
            )
    stacked = jnp.stack(tap_list)
    return stacked.reshape(-1, stacked.shape[2])


def back_terms(padded, weight, row_count, rim_start):
    accumulated = None
    for row_offset in (-1, 0, 1):
        for col_offset in (-1, 0, 1):
            shifted_piece = shifted(padded, row_offset, col_offset, row_count, rim_start)
            product = lax.dot_general(
                shifted_piece,
                weight[row_offset + 1, col_offset + 1],
                (((3,), (1,)), ((), ())),
                preferred_element_type=jnp.float32,
            )
            accumulated = product if accumulated is None else accumulated + product
    return accumulated


def swap(array, axis, step):
    peers = lax.axis_size(axis)
    return lax.ppermute(array, axis, [(i, i ^ step) for i in range(peers)])


def halve_step(blocks, axis, bit, dim, split=True):
    own = (lax.axis_index(axis) >> bit) & 1
    keep = lax.dynamic_index_in_dim(blocks, own, axis=dim, keepdims=False)
    give = lax.dynamic_index_in_dim(blocks, 1 - own, axis=dim, keepdims=False)
    half = give.shape[0] // 2
    if half == 0 or not split:
        return keep + swap(give, axis, 1 << bit)
    got = [swap(give[:half], axis, 1 << bit), swap(give[half:], axis, 1 << bit)]
    return keep + jnp.concatenate(got, axis=0)


def settle_stages(grad_scale):
    dates, bands = lax.axis_size("date"), lax.axis_size("band")
    band_bits, date_bits = bands.bit_length() - 1, dates.bit_length() - 1
    stages = []

    def start(grad_term):
        rows, cols = grad_term.shape
        piece = rows // (dates * bands)
        blocks = grad_term.reshape((dates,) + (2,) * band_bits + (piece, cols))
        half = dates // 2
        return tuple(halve_step(part, "band", 0, 1, split=False) for part in (blocks[:half], blocks[half:]))

    stages.append((start, True))
    orders = [list(range(1, band_bits)), list(range(band_bits - 1, 0, -1))]

    for step in range(band_bits - 1):

        def band_step(parts, step=step):
            moved = []
            for part, order in zip(parts, orders):
                bit = order[step]
                done = order[:step]
                left = [b for b in range(1, band_bits) if b not in done]
                moved.append(halve_step(part, "band", bit, 1 + left.index(bit)))
            return tuple(moved)

        stages.append((band_step, True))
    def to_dates(parts):
        return tuple(p.reshape((2,) * (date_bits - 1) + p.shape[-2:]) for p in parts)

    stages.append((to_dates, False))
    for bit in range(date_bits - 1):

        def low_step(parts, bit=bit):
            return tuple(halve_step(p, "date", bit, date_bits - 2 - bit) for p in parts)

        stages.append((low_step, True))

    def top_step(parts):
        blocks = jnp.stack(parts, axis=0)
        return halve_step(blocks, "date", date_bits - 1, 0)

    stages.append((top_step, True))
    stages.append((lambda block: block * grad_scale, False))
    if band_bits > 1:

        def gather_far(block):
            mine = lax.axis_index("band") >> 1
            count = 1 << (band_bits - 1)
            got = [block] + [swap(block, "band", m << 1) for m in range(1, count)]
            placed = []
            for spot in range(count):
                owner = int(format(spot, "0%db" % (band_bits - 1))[::-1], 2)
                pick = got[0]
                for m in range(1, count):
                    pick = jnp.where((mine ^ m) == owner, got[m], pick)
                placed.append(pick)
            return jnp.stack(placed, axis=0).reshape((2,) * (band_bits - 1) + block.shape)

        stages.append((gather_far, True))

    def gather_near(block):
        other = swap(block, "band", 1)
        low = (lax.axis_index("band") & 1) == 0
        return jnp.stack([jnp.where(low, block, other), jnp.where(low, other, block)], axis=0)

    stages.append((gather_near, True))
    return stages


class Chain:
    def __init__(self, stages, state):
        self.stages, self.state, self.at = stages, state, 0

    def advance(self, count):
        while count > 0 and self.at < len(self.stages):
            stage, sends = self.stages[self.at]
            self.state = stage(self.state)
            self.at += 1
            count -= int(sends)

    def tie(self, value):
        self.state, value = lax.optimization_barrier((self.state, value))
        return value

    def finish(self, rows, cols):
        self.advance(len(self.stages))
        return self.state.reshape(rows, cols)


def tie_chains(first, second):
    first.state, second.state = lax.optimization_barrier((first.state, second.state))


def body(inputs, preact_one, preact_two, cotangent, weight_one, weight_two):
    row_count = inputs.shape[1]
    grad_scale = 1.0 / (inputs.shape[0] * lax.axis_size("date"))
    act_one = jax.nn.silu(preact_one.astype(jnp.float32)).astype(jnp.bfloat16)
    delta_two = (cotangent.astype(jnp.float32) * slope(preact_two.astype(jnp.float32))).astype(
        jnp.bfloat16
    )
    padded_two = pad_columns(extended(delta_two, (("band", 1),), 1))
    term_two = weight_terms(act_one, padded_two, 1)
    out_rows = term_two.shape[0] // lax.axis_size("date")
    back_one = back_terms(padded_two, weight_two, row_count, 1)
    delta_one = (back_one * slope(preact_one.astype(jnp.float32))).astype(jnp.bfloat16)
    padded_one = pad_columns(extended(delta_one, (("band", 1),), 1))
    term_one = weight_terms(inputs, padded_one, 1)
    input_grad = back_terms(padded_one, weight_one, row_count, 1).astype(jnp.bfloat16)
    band_sends = lax.axis_size("band").bit_length() - 1
    date_sends = lax.axis_size("date").bit_length() - 1
    two = Chain(settle_stages(grad_scale), term_two)
    one = Chain(settle_stages(grad_scale), term_one)
    two.advance(band_sends)
    one.advance(1)
    tie_chains(two, one)
    two.advance(date_sends)
    one.advance(band_sends - 1)
    tie_chains(two, one)
    grad_two = two.finish(out_rows, term_two.shape[1])
    grad_one = one.finish(out_rows, term_one.shape[1])
    return (input_grad, grad_one, grad_two)


def solution(mesh):
    placed = (
        P("date", "band", None, None),
        P("date", "band", None, None),
        P("date", "band", None, None),
        P("date", "band", None, None),
        P(),
        P(),
    )
    return jax.shard_map(
        body,
        mesh=mesh,
        in_specs=placed,
        out_specs=(P("date", "band", None, None), P("date", None), P("date", None)),
        check_vma=False,
    )
```

```python
import jax
import jax.numpy as jnp
from jax import lax
from jax.sharding import PartitionSpec as P


def extended(array, sides, width):
    for axis, dim in sides:
        peers, length = (lax.axis_size(axis), array.shape[dim])
        up = [(i, (i + 1) % peers) for i in range(peers - 1)]
        down = [(j, i) for i, j in up]
        last = lax.slice_in_dim(array, length - width, length, axis=dim)
        leading = lax.slice_in_dim(array, 0, width, axis=dim)
        before = lax.ppermute(last, axis, up)
        after = lax.ppermute(leading, axis, down)
        array = jnp.concatenate([before, array, after], axis=dim)
    return array


def slope(field_value):
    logistic = jax.nn.sigmoid(field_value)
    return logistic * (1.0 + field_value * (1.0 - logistic))


def pad_columns(field_value):
    return jnp.pad(field_value, ((0, 0), (0, 0), (1, 1), (0, 0)))


def shifted(padded, row_offset, col_offset, row_count, rim_start):
    col_count = padded.shape[2] - 2
    return padded[
        :,
        rim_start - row_offset : rim_start - row_offset + row_count,
        1 - col_offset : 1 - col_offset + col_count,
        :,
    ]


def weight_terms(left_field, padded, rim_start):
    row_count = left_field.shape[1]
    tap_list = []
    for row_offset in (-1, 0, 1):
        for col_offset in (-1, 0, 1):
            shifted_piece = shifted(padded, row_offset, col_offset, row_count, rim_start)
            tap_list.append(
                lax.dot_general(
                    left_field,
                    shifted_piece,
                    (((0, 1, 2), (0, 1, 2)), ((), ())),
                    preferred_element_type=jnp.float32,
                )
            )
    stacked = jnp.stack(tap_list)
    return stacked.reshape(-1, stacked.shape[2])


def back_terms(padded, weight, row_count, rim_start):
    accumulated = None
    for row_offset in (-1, 0, 1):
        for col_offset in (-1, 0, 1):
            shifted_piece = shifted(padded, row_offset, col_offset, row_count, rim_start)
            product = lax.dot_general(
                shifted_piece,
                weight[row_offset + 1, col_offset + 1],
                (((3,), (1,)), ((), ())),
                preferred_element_type=jnp.float32,
            )
            accumulated = product if accumulated is None else accumulated + product
    return accumulated


def swap(array, axis, step):
    peers = lax.axis_size(axis)
    return lax.ppermute(array, axis, [(i, i ^ step) for i in range(peers)])


def halve_step(blocks, axis, bit, dim):
    own = (lax.axis_index(axis) >> bit) & 1
    keep = lax.dynamic_index_in_dim(blocks, own, axis=dim, keepdims=False)
    give = lax.dynamic_index_in_dim(blocks, 1 - own, axis=dim, keepdims=False)
    half = give.shape[0] // 2
    if half == 0:
        return keep + swap(give, axis, 1 << bit)
    got = [swap(give[:half], axis, 1 << bit), swap(give[half:], axis, 1 << bit)]
    return keep + jnp.concatenate(got, axis=0)


def settle_stages(grad_scale):
    dates, bands = lax.axis_size("date"), lax.axis_size("band")
    band_bits, date_bits = bands.bit_length() - 1, dates.bit_length() - 1
    stages = []

    def start(grad_term):
        rows, cols = grad_term.shape
        piece = rows // (dates * bands)
        blocks = grad_term.reshape((dates,) + (2,) * band_bits + (piece, cols))
        return halve_step(blocks, "band", 0, 1)

    stages.append((start, True))
    orders = [list(range(1, band_bits)), list(range(band_bits - 1, 0, -1))]

    def split(blocks):
        half = blocks.shape[0] // 2
        return (blocks[:half], blocks[half:])

    if band_bits > 1:
        stages.append((split, False))
    for step in range(band_bits - 1):

        def band_step(parts, step=step):
            moved = []
            for part, order in zip(parts, orders):
                bit = order[step]
                done = order[:step]
                left = [b for b in range(1, band_bits) if b not in done]
                moved.append(halve_step(part, "band", bit, 1 + left.index(bit)))
            return tuple(moved)

        stages.append((band_step, True))
    def to_dates(parts):
        return tuple(p.reshape((2,) * (date_bits - 1) + p.shape[-2:]) for p in parts)

    stages.append((to_dates, False))
    for bit in range(date_bits - 1):

        def low_step(parts, bit=bit):
            return tuple(halve_step(p, "date", bit, date_bits - 2 - bit) for p in parts)

        stages.append((low_step, True))

    def top_step(parts):
        blocks = jnp.stack(parts, axis=0)
        return halve_step(blocks, "date", date_bits - 1, 0)

    stages.append((top_step, True))
    stages.append((lambda block: block * grad_scale, False))
    if band_bits > 1:

        def gather_far(block):
            mine = lax.axis_index("band") >> 1
            count = 1 << (band_bits - 1)
            got = [block] + [swap(block, "band", m << 1) for m in range(1, count)]
            placed = []
            for spot in range(count):
                owner = int(format(spot, "0%db" % (band_bits - 1))[::-1], 2)
                pick = got[0]
                for m in range(1, count):
                    pick = jnp.where((mine ^ m) == owner, got[m], pick)
                placed.append(pick)
            return jnp.stack(placed, axis=0).reshape((2,) * (band_bits - 1) + block.shape)

        stages.append((gather_far, True))

    def gather_near(block):
        other = swap(block, "band", 1)
        low = (lax.axis_index("band") & 1) == 0
        return jnp.stack([jnp.where(low, block, other), jnp.where(low, other, block)], axis=0)

    stages.append((gather_near, True))
    return stages


class Chain:
    def __init__(self, stages, state):
        self.stages, self.state, self.at = stages, state, 0

    def advance(self, count):
        while count > 0 and self.at < len(self.stages):
            stage, sends = self.stages[self.at]
            self.state = stage(self.state)
            self.at += 1
            count -= int(sends)

    def tie(self, value):
        self.state, value = lax.optimization_barrier((self.state, value))
        return value

    def finish(self, rows, cols):
        self.advance(len(self.stages))
        return self.state.reshape(rows, cols)


def tie_chains(first, second):
    first.state, second.state = lax.optimization_barrier((first.state, second.state))


def body(inputs, preact_one, preact_two, cotangent, weight_one, weight_two):
    row_count = inputs.shape[1]
    grad_scale = 1.0 / (inputs.shape[0] * lax.axis_size("date"))
    act_one = jax.nn.silu(preact_one.astype(jnp.float32)).astype(jnp.bfloat16)
    delta_two = (cotangent.astype(jnp.float32) * slope(preact_two.astype(jnp.float32))).astype(
        jnp.bfloat16
    )
    padded_two = pad_columns(extended(delta_two, (("band", 1),), 1))
    term_two = weight_terms(act_one, padded_two, 1)
    out_rows = term_two.shape[0] // lax.axis_size("date")
    back_one = back_terms(padded_two, weight_two, row_count, 1)
    delta_one = (back_one * slope(preact_one.astype(jnp.float32))).astype(jnp.bfloat16)
    padded_one = pad_columns(extended(delta_one, (("band", 1),), 1))
    term_one = weight_terms(inputs, padded_one, 1)
    input_grad = back_terms(padded_one, weight_one, row_count, 1).astype(jnp.bfloat16)
    band_sends = lax.axis_size("band").bit_length() - 1
    date_sends = lax.axis_size("date").bit_length() - 1
    two = Chain(settle_stages(grad_scale), term_two)
    one = Chain(settle_stages(grad_scale), term_one)
    two.advance(band_sends)
    tie_chains(two, one)
    one.advance(1)
    two.advance(date_sends)
    one.advance(band_sends - 1)
    tie_chains(two, one)
    grad_two = two.finish(out_rows, term_two.shape[1])
    grad_one = one.finish(out_rows, term_one.shape[1])
    return (input_grad, grad_one, grad_two)


def solution(mesh):
    placed = (
        P("date", "band", None, None),
        P("date", "band", None, None),
        P("date", "band", None, None),
        P("date", "band", None, None),
        P(),
        P(),
    )
    return jax.shard_map(
        body,
        mesh=mesh,
        in_specs=placed,
        out_specs=(P("date", "band", None, None), P("date", None), P("date", None)),
        check_vma=False,
    )
```

```python
import jax
import jax.numpy as jnp
from jax import lax
from jax.sharding import PartitionSpec as P


def extended(array, sides, width):
    for axis, dim in sides:
        peers, length = (lax.axis_size(axis), array.shape[dim])
        up = [(i, (i + 1) % peers) for i in range(peers - 1)]
        down = [(j, i) for i, j in up]
        last = lax.slice_in_dim(array, length - width, length, axis=dim)
        leading = lax.slice_in_dim(array, 0, width, axis=dim)
        before = lax.ppermute(last, axis, up)
        after = lax.ppermute(leading, axis, down)
        array = jnp.concatenate([before, array, after], axis=dim)
    return array


def slope(field_value):
    logistic = jax.nn.sigmoid(field_value)
    return logistic * (1.0 + field_value * (1.0 - logistic))


def pad_columns(field_value):
    return jnp.pad(field_value, ((0, 0), (0, 0), (1, 1), (0, 0)))


def shifted(padded, row_offset, col_offset, row_count, rim_start):
    col_count = padded.shape[2] - 2
    return padded[
        :,
        rim_start - row_offset : rim_start - row_offset + row_count,
        1 - col_offset : 1 - col_offset + col_count,
        :,
    ]


def weight_terms(left_field, padded, rim_start):
    row_count = left_field.shape[1]
    tap_list = []
    for row_offset in (-1, 0, 1):
        for col_offset in (-1, 0, 1):
            shifted_piece = shifted(padded, row_offset, col_offset, row_count, rim_start)
            tap_list.append(
                lax.dot_general(
                    left_field,
                    shifted_piece,
                    (((0, 1, 2), (0, 1, 2)), ((), ())),
                    preferred_element_type=jnp.float32,
                )
            )
    stacked = jnp.stack(tap_list)
    return stacked.reshape(-1, stacked.shape[2])


def back_terms(padded, weight, row_count, rim_start):
    accumulated = None
    for row_offset in (-1, 0, 1):
        for col_offset in (-1, 0, 1):
            shifted_piece = shifted(padded, row_offset, col_offset, row_count, rim_start)
            product = lax.dot_general(
                shifted_piece,
                weight[row_offset + 1, col_offset + 1],
                (((3,), (1,)), ((), ())),
                preferred_element_type=jnp.float32,
            )
            accumulated = product if accumulated is None else accumulated + product
    return accumulated


def swap(array, axis, step):
    peers = lax.axis_size(axis)
    return lax.ppermute(array, axis, [(i, i ^ step) for i in range(peers)])


def halve_step(blocks, axis, bit, dim):
    own = (lax.axis_index(axis) >> bit) & 1
    keep = lax.dynamic_index_in_dim(blocks, own, axis=dim, keepdims=False)
    give = lax.dynamic_index_in_dim(blocks, 1 - own, axis=dim, keepdims=False)
    half = give.shape[0] // 2
    if half == 0:
        return keep + swap(give, axis, 1 << bit)
    got = [swap(give[:half], axis, 1 << bit), swap(give[half:], axis, 1 << bit)]
    return keep + jnp.concatenate(got, axis=0)


def settle_stages(grad_scale):
    dates, bands = lax.axis_size("date"), lax.axis_size("band")
    band_bits, date_bits = bands.bit_length() - 1, dates.bit_length() - 1
    stages = []

    def start(grad_term):
        rows, cols = grad_term.shape
        piece = rows // (dates * bands)
        blocks = grad_term.reshape((dates,) + (2,) * band_bits + (piece, cols))
        return halve_step(blocks, "band", 0, 1)

    stages.append((start, True))
    orders = [list(range(1, band_bits)), list(range(band_bits - 1, 0, -1))]

    def split(blocks):
        half = blocks.shape[0] // 2
        return (blocks[:half], blocks[half:])

    if band_bits > 1:
        stages.append((split, False))
    for step in range(band_bits - 1):

        def band_step(parts, step=step):
            moved = []
            for part, order in zip(parts, orders):
                bit = order[step]
                done = order[:step]
                left = [b for b in range(1, band_bits) if b not in done]
                moved.append(halve_step(part, "band", bit, 1 + left.index(bit)))
            return tuple(moved)

        stages.append((band_step, True))
    def to_dates(parts):
        return tuple(p.reshape((2,) * (date_bits - 1) + p.shape[-2:]) for p in parts)

    stages.append((to_dates, False))
    for bit in range(date_bits - 1):

        def low_step(parts, bit=bit):
            return tuple(halve_step(p, "date", bit, date_bits - 2 - bit) for p in parts)

        stages.append((low_step, True))

    def top_step(parts):
        blocks = jnp.stack(parts, axis=0)
        return halve_step(blocks, "date", date_bits - 1, 0)

    stages.append((top_step, True))
    stages.append((lambda block: block * grad_scale, False))
    if band_bits > 1:

        def gather_far(block):
            mine = lax.axis_index("band") >> 1
            count = 1 << (band_bits - 1)
            got = [block] + [swap(block, "band", m << 1) for m in range(1, count)]
            placed = []
            for spot in range(count):
                owner = int(format(spot, "0%db" % (band_bits - 1))[::-1], 2)
                pick = got[0]
                for m in range(1, count):
                    pick = jnp.where((mine ^ m) == owner, got[m], pick)
                placed.append(pick)
            return jnp.stack(placed, axis=0).reshape((2,) * (band_bits - 1) + block.shape)

        stages.append((gather_far, True))

    def gather_near(block):
        other = swap(block, "band", 1)
        low = (lax.axis_index("band") & 1) == 0
        return jnp.stack([jnp.where(low, block, other), jnp.where(low, other, block)], axis=0)

    stages.append((gather_near, True))
    return stages


class Chain:
    def __init__(self, stages, state):
        self.stages, self.state, self.at = stages, state, 0

    def advance(self, count):
        while count > 0 and self.at < len(self.stages):
            stage, sends = self.stages[self.at]
            self.state = stage(self.state)
            self.at += 1
            count -= int(sends)

    def tie(self, value):
        self.state, value = lax.optimization_barrier((self.state, value))
        return value

    def finish(self, rows, cols):
        self.advance(len(self.stages))
        return self.state.reshape(rows, cols)


def tie_chains(first, second):
    first.state, second.state = lax.optimization_barrier((first.state, second.state))


def body(inputs, preact_one, preact_two, cotangent, weight_one, weight_two):
    row_count = inputs.shape[1]
    grad_scale = 1.0 / (inputs.shape[0] * lax.axis_size("date"))
    act_one = jax.nn.silu(preact_one.astype(jnp.float32)).astype(jnp.bfloat16)
    delta_two = (cotangent.astype(jnp.float32) * slope(preact_two.astype(jnp.float32))).astype(
        jnp.bfloat16
    )
    padded_two = pad_columns(extended(delta_two, (("band", 1),), 1))
    term_two = weight_terms(act_one, padded_two, 1)
    out_rows = term_two.shape[0] // lax.axis_size("date")
    back_one = back_terms(padded_two, weight_two, row_count, 1)
    delta_one = (back_one * slope(preact_one.astype(jnp.float32))).astype(jnp.bfloat16)
    padded_one = pad_columns(extended(delta_one, (("band", 1),), 1))
    term_one = weight_terms(inputs, padded_one, 1)
    input_grad = back_terms(padded_one, weight_one, row_count, 1).astype(jnp.bfloat16)
    band_sends = lax.axis_size("band").bit_length() - 1
    date_sends = lax.axis_size("date").bit_length() - 1
    two = Chain(settle_stages(grad_scale), term_two)
    one = Chain(settle_stages(grad_scale), term_one)
    two.advance(band_sends)
    one.advance(1)
    tie_chains(two, one)
    two.advance(date_sends)
    one.advance(band_sends - 1)
    grad_two = two.finish(out_rows, term_two.shape[1])
    grad_one = one.finish(out_rows, term_one.shape[1])
    return (input_grad, grad_one, grad_two)


def solution(mesh):
    placed = (
        P("date", "band", None, None),
        P("date", "band", None, None),
        P("date", "band", None, None),
        P("date", "band", None, None),
        P(),
        P(),
    )
    return jax.shard_map(
        body,
        mesh=mesh,
        in_specs=placed,
        out_specs=(P("date", "band", None, None), P("date", None), P("date", None)),
        check_vma=False,
    )
```

```python
import jax
import jax.numpy as jnp
from jax import lax
from jax.sharding import PartitionSpec as P


def extended(array, sides, width):
    for axis, dim in sides:
        peers, length = (lax.axis_size(axis), array.shape[dim])
        up = [(i, (i + 1) % peers) for i in range(peers - 1)]
        down = [(j, i) for i, j in up]
        last = lax.slice_in_dim(array, length - width, length, axis=dim)
        leading = lax.slice_in_dim(array, 0, width, axis=dim)
        before = lax.ppermute(last, axis, up)
        after = lax.ppermute(leading, axis, down)
        array = jnp.concatenate([before, array, after], axis=dim)
    return array


def slope(field_value):
    logistic = jax.nn.sigmoid(field_value)
    return logistic * (1.0 + field_value * (1.0 - logistic))


def pad_columns(field_value):
    return jnp.pad(field_value, ((0, 0), (0, 0), (1, 1), (0, 0)))


def shifted(padded, row_offset, col_offset, row_count, rim_start):
    col_count = padded.shape[2] - 2
    return padded[
        :,
        rim_start - row_offset : rim_start - row_offset + row_count,
        1 - col_offset : 1 - col_offset + col_count,
        :,
    ]


def weight_terms(left_field, padded, rim_start):
    row_count = left_field.shape[1]
    tap_list = []
    for row_offset in (-1, 0, 1):
        for col_offset in (-1, 0, 1):
            shifted_piece = shifted(padded, row_offset, col_offset, row_count, rim_start)
            tap_list.append(
                lax.dot_general(
                    left_field,
                    shifted_piece,
                    (((0, 1, 2), (0, 1, 2)), ((), ())),
                    preferred_element_type=jnp.float32,
                )
            )
    stacked = jnp.stack(tap_list)
    return stacked.reshape(-1, stacked.shape[2])


def back_terms(padded, weight, row_count, rim_start):
    accumulated = None
    for row_offset in (-1, 0, 1):
        for col_offset in (-1, 0, 1):
            shifted_piece = shifted(padded, row_offset, col_offset, row_count, rim_start)
            product = lax.dot_general(
                shifted_piece,
                weight[row_offset + 1, col_offset + 1],
                (((3,), (1,)), ((), ())),
                preferred_element_type=jnp.float32,
            )
            accumulated = product if accumulated is None else accumulated + product
    return accumulated


def swap(array, axis, step):
    peers = lax.axis_size(axis)
    return lax.ppermute(array, axis, [(i, i ^ step) for i in range(peers)])


def halve_step(blocks, axis, bit, dim):
    own = (lax.axis_index(axis) >> bit) & 1
    keep = lax.dynamic_index_in_dim(blocks, own, axis=dim, keepdims=False)
    give = lax.dynamic_index_in_dim(blocks, 1 - own, axis=dim, keepdims=False)
    half = give.shape[0] // 2
    if half == 0:
        return keep + swap(give, axis, 1 << bit)
    got = [swap(give[:half], axis, 1 << bit), swap(give[half:], axis, 1 << bit)]
    return keep + jnp.concatenate(got, axis=0)


def settle_stages(grad_scale):
    dates, bands = lax.axis_size("date"), lax.axis_size("band")
    band_bits, date_bits = bands.bit_length() - 1, dates.bit_length() - 1
    stages = []

    def start(grad_term):
        rows, cols = grad_term.shape
        piece = rows // (dates * bands)
        blocks = grad_term.reshape((dates,) + (2,) * band_bits + (piece, cols))
        return halve_step(blocks, "band", 0, 1)

    stages.append((start, True))
    orders = [list(range(1, band_bits)), list(range(band_bits - 1, 0, -1))]

    def split(blocks):
        half = blocks.shape[0] // 2
        return (blocks[:half], blocks[half:])

    if band_bits > 1:
        stages.append((split, False))
    for step in range(band_bits - 1):

        def band_step(parts, step=step):
            moved = []
            for part, order in zip(parts, orders):
                bit = order[step]
                done = order[:step]
                left = [b for b in range(1, band_bits) if b not in done]
                moved.append(halve_step(part, "band", bit, 1 + left.index(bit)))
            return tuple(moved)

        stages.append((band_step, True))
    def to_dates(parts):
        return tuple(p.reshape((2,) * (date_bits - 1) + p.shape[-2:]) for p in parts)

    stages.append((to_dates, False))
    for bit in range(date_bits - 1):

        def low_step(parts, bit=bit):
            return tuple(halve_step(p, "date", bit, date_bits - 2 - bit) for p in parts)

        stages.append((low_step, True))

    def top_step(parts):
        blocks = jnp.stack(parts, axis=0)
        return halve_step(blocks, "date", date_bits - 1, 0)

    stages.append((top_step, True))
    stages.append((lambda block: block * grad_scale, False))
    if band_bits > 1:

        def gather_far(block):
            mine = lax.axis_index("band") >> 1
            count = 1 << (band_bits - 1)
            got = [block] + [swap(block, "band", m << 1) for m in range(1, count)]
            placed = []
            for spot in range(count):
                owner = int(format(spot, "0%db" % (band_bits - 1))[::-1], 2)
                pick = got[0]
                for m in range(1, count):
                    pick = jnp.where((mine ^ m) == owner, got[m], pick)
                placed.append(pick)
            return jnp.stack(placed, axis=0).reshape((2,) * (band_bits - 1) + block.shape)

        stages.append((gather_far, True))

    def gather_near(block):
        other = swap(block, "band", 1)
        low = (lax.axis_index("band") & 1) == 0
        return jnp.stack([jnp.where(low, block, other), jnp.where(low, other, block)], axis=0)

    stages.append((gather_near, True))
    return stages


class Chain:
    def __init__(self, stages, state):
        self.stages, self.state, self.at = stages, state, 0

    def advance(self, count):
        while count > 0 and self.at < len(self.stages):
            stage, sends = self.stages[self.at]
            self.state = stage(self.state)
            self.at += 1
            count -= int(sends)

    def tie(self, value):
        self.state, value = lax.optimization_barrier((self.state, value))
        return value

    def finish(self, rows, cols):
        self.advance(len(self.stages))
        return self.state.reshape(rows, cols)


def tie_chains(first, second):
    first.state, second.state = lax.optimization_barrier((first.state, second.state))


def body(inputs, preact_one, preact_two, cotangent, weight_one, weight_two):
    row_count = inputs.shape[1]
    grad_scale = 1.0 / (inputs.shape[0] * lax.axis_size("date"))
    act_one = jax.nn.silu(preact_one.astype(jnp.float32)).astype(jnp.bfloat16)
    delta_two = (cotangent.astype(jnp.float32) * slope(preact_two.astype(jnp.float32))).astype(
        jnp.bfloat16
    )
    padded_two = pad_columns(extended(delta_two, (("band", 1),), 1))
    term_two = weight_terms(act_one, padded_two, 1)
    out_rows = term_two.shape[0] // lax.axis_size("date")
    back_one = back_terms(padded_two, weight_two, row_count, 1)
    delta_one = (back_one * slope(preact_one.astype(jnp.float32))).astype(jnp.bfloat16)
    padded_one = pad_columns(extended(delta_one, (("band", 1),), 1))
    term_one = weight_terms(inputs, padded_one, 1)
    input_grad = back_terms(padded_one, weight_one, row_count, 1).astype(jnp.bfloat16)
    band_sends = lax.axis_size("band").bit_length() - 1
    date_sends = lax.axis_size("date").bit_length() - 1
    two = Chain(settle_stages(grad_scale), term_two)
    one = Chain(settle_stages(grad_scale), term_one)
    two.advance(band_sends - 1)
    one.advance(1)
    tie_chains(two, one)
    two.advance(1 + date_sends)
    one.advance(band_sends - 1)
    tie_chains(two, one)
    grad_two = two.finish(out_rows, term_two.shape[1])
    grad_one = one.finish(out_rows, term_one.shape[1])
    return (input_grad, grad_one, grad_two)


def solution(mesh):
    placed = (
        P("date", "band", None, None),
        P("date", "band", None, None),
        P("date", "band", None, None),
        P("date", "band", None, None),
        P(),
        P(),
    )
    return jax.shard_map(
        body,
        mesh=mesh,
        in_specs=placed,
        out_specs=(P("date", "band", None, None), P("date", None), P("date", None)),
        check_vma=False,
    )
```

```python
import jax
import jax.numpy as jnp
from jax import lax
from jax.sharding import PartitionSpec as P


def extended(array, sides, width):
    for axis, dim in sides:
        peers, length = (lax.axis_size(axis), array.shape[dim])
        up = [(i, (i + 1) % peers) for i in range(peers - 1)]
        down = [(j, i) for i, j in up]
        last = lax.slice_in_dim(array, length - width, length, axis=dim)
        leading = lax.slice_in_dim(array, 0, width, axis=dim)
        before = lax.ppermute(last, axis, up)
        after = lax.ppermute(leading, axis, down)
        array = jnp.concatenate([before, array, after], axis=dim)
    return array


def slope(field_value):
    logistic = jax.nn.sigmoid(field_value)
    return logistic * (1.0 + field_value * (1.0 - logistic))


def pad_columns(field_value):
    return jnp.pad(field_value, ((0, 0), (0, 0), (1, 1), (0, 0)))


def shifted(padded, row_offset, col_offset, row_count, rim_start):
    col_count = padded.shape[2] - 2
    return padded[
        :,
        rim_start - row_offset : rim_start - row_offset + row_count,
        1 - col_offset : 1 - col_offset + col_count,
        :,
    ]


def weight_terms(left_field, padded, rim_start):
    row_count = left_field.shape[1]
    tap_list = []
    for row_offset in (-1, 0, 1):
        for col_offset in (-1, 0, 1):
            shifted_piece = shifted(padded, row_offset, col_offset, row_count, rim_start)
            tap_list.append(
                lax.dot_general(
                    left_field,
                    shifted_piece,
                    (((0, 1, 2), (0, 1, 2)), ((), ())),
                    preferred_element_type=jnp.float32,
                )
            )
    stacked = jnp.stack(tap_list)
    return stacked.reshape(-1, stacked.shape[2])


def back_terms(padded, weight, row_count, rim_start):
    accumulated = None
    for row_offset in (-1, 0, 1):
        for col_offset in (-1, 0, 1):
            shifted_piece = shifted(padded, row_offset, col_offset, row_count, rim_start)
            product = lax.dot_general(
                shifted_piece,
                weight[row_offset + 1, col_offset + 1],
                (((3,), (1,)), ((), ())),
                preferred_element_type=jnp.float32,
            )
            accumulated = product if accumulated is None else accumulated + product
    return accumulated


def swap(array, axis, step):
    peers = lax.axis_size(axis)
    return lax.ppermute(array, axis, [(i, i ^ step) for i in range(peers)])


def halve_step(blocks, axis, bit, dim):
    own = (lax.axis_index(axis) >> bit) & 1
    keep = lax.dynamic_index_in_dim(blocks, own, axis=dim, keepdims=False)
    give = lax.dynamic_index_in_dim(blocks, 1 - own, axis=dim, keepdims=False)
    half = give.shape[0] // 2
    if half == 0:
        return keep + swap(give, axis, 1 << bit)
    got = [swap(give[:half], axis, 1 << bit), swap(give[half:], axis, 1 << bit)]
    return keep + jnp.concatenate(got, axis=0)


def settle_stages(grad_scale):
    dates, bands = lax.axis_size("date"), lax.axis_size("band")
    band_bits, date_bits = bands.bit_length() - 1, dates.bit_length() - 1
    stages = []

    def start(grad_term):
        rows, cols = grad_term.shape
        piece = rows // (dates * bands)
        blocks = grad_term.reshape((dates,) + (2,) * band_bits + (piece, cols))
        return halve_step(blocks, "band", 0, 1)

    stages.append((start, True))
    orders = [list(range(1, band_bits)), list(range(band_bits - 1, 0, -1))]

    def split(blocks):
        half = blocks.shape[0] // 2
        return (blocks[:half], blocks[half:])

    if band_bits > 1:
        stages.append((split, False))
    for step in range(band_bits - 1):

        def band_step(parts, step=step):
            moved = []
            for part, order in zip(parts, orders):
                bit = order[step]
                done = order[:step]
                left = [b for b in range(1, band_bits) if b not in done]
                moved.append(halve_step(part, "band", bit, 1 + left.index(bit)))
            return tuple(moved)

        stages.append((band_step, True))
    def to_dates(parts):
        return tuple(p.reshape((2,) * (date_bits - 1) + p.shape[-2:]) for p in parts)

    stages.append((to_dates, False))
    for bit in range(date_bits - 1):

        def low_step(parts, bit=bit):
            return tuple(halve_step(p, "date", bit, date_bits - 2 - bit) for p in parts)

        stages.append((low_step, True))

    def top_step(parts):
        blocks = jnp.stack(parts, axis=0)
        return halve_step(blocks, "date", date_bits - 1, 0)

    stages.append((top_step, True))
    stages.append((lambda block: block * grad_scale, False))
    if band_bits > 1:

        def gather_far(block):
            mine = lax.axis_index("band") >> 1
            count = 1 << (band_bits - 1)
            got = [block] + [swap(block, "band", m << 1) for m in range(1, count)]
            placed = []
            for spot in range(count):
                owner = int(format(spot, "0%db" % (band_bits - 1))[::-1], 2)
                pick = got[0]
                for m in range(1, count):
                    pick = jnp.where((mine ^ m) == owner, got[m], pick)
                placed.append(pick)
            return jnp.stack(placed, axis=0).reshape((2,) * (band_bits - 1) + block.shape)

        stages.append((gather_far, True))

    def gather_near(block):
        other = swap(block, "band", 1)
        low = (lax.axis_index("band") & 1) == 0
        return jnp.stack([jnp.where(low, block, other), jnp.where(low, other, block)], axis=0)

    stages.append((gather_near, True))
    return stages


class Chain:
    def __init__(self, stages, state):
        self.stages, self.state, self.at = stages, state, 0

    def advance(self, count):
        while count > 0 and self.at < len(self.stages):
            stage, sends = self.stages[self.at]
            self.state = stage(self.state)
            self.at += 1
            count -= int(sends)

    def tie(self, value):
        self.state, value = lax.optimization_barrier((self.state, value))
        return value

    def finish(self, rows, cols):
        self.advance(len(self.stages))
        return self.state.reshape(rows, cols)


def tie_chains(first, second):
    first.state, second.state = lax.optimization_barrier((first.state, second.state))


def body(inputs, preact_one, preact_two, cotangent, weight_one, weight_two):
    row_count = inputs.shape[1]
    grad_scale = 1.0 / (inputs.shape[0] * lax.axis_size("date"))
    act_one = jax.nn.silu(preact_one.astype(jnp.float32)).astype(jnp.bfloat16)
    delta_two = (cotangent.astype(jnp.float32) * slope(preact_two.astype(jnp.float32))).astype(
        jnp.bfloat16
    )
    padded_two = pad_columns(extended(delta_two, (("band", 1),), 1))
    term_two = weight_terms(act_one, padded_two, 1)
    out_rows = term_two.shape[0] // lax.axis_size("date")
    back_one = back_terms(padded_two, weight_two, row_count, 1)
    delta_one = (back_one * slope(preact_one.astype(jnp.float32))).astype(jnp.bfloat16)
    padded_one = pad_columns(extended(delta_one, (("band", 1),), 1))
    term_one = weight_terms(inputs, padded_one, 1)
    input_grad = back_terms(padded_one, weight_one, row_count, 1).astype(jnp.bfloat16)
    band_sends = lax.axis_size("band").bit_length() - 1
    date_sends = lax.axis_size("date").bit_length() - 1
    two = Chain(settle_stages(grad_scale), term_two)
    one = Chain(settle_stages(grad_scale), term_one)
    two.advance(band_sends)
    one.advance(1)
    tie_chains(two, one)
    two.advance(date_sends + 1)
    one.advance(band_sends - 1)
    tie_chains(two, one)
    grad_two = two.finish(out_rows, term_two.shape[1])
    grad_one = one.finish(out_rows, term_one.shape[1])
    return (input_grad, grad_one, grad_two)


def solution(mesh):
    placed = (
        P("date", "band", None, None),
        P("date", "band", None, None),
        P("date", "band", None, None),
        P("date", "band", None, None),
        P(),
        P(),
    )
    return jax.shard_map(
        body,
        mesh=mesh,
        in_specs=placed,
        out_specs=(P("date", "band", None, None), P("date", None), P("date", None)),
        check_vma=False,
    )
```

```python
import jax
import jax.numpy as jnp
from jax import lax
from jax.sharding import PartitionSpec as P


def extended(array, sides, width):
    for axis, dim in sides:
        peers, length = (lax.axis_size(axis), array.shape[dim])
        up = [(i, (i + 1) % peers) for i in range(peers - 1)]
        down = [(j, i) for i, j in up]
        last = lax.slice_in_dim(array, length - width, length, axis=dim)
        leading = lax.slice_in_dim(array, 0, width, axis=dim)
        before = lax.ppermute(last, axis, up)
        after = lax.ppermute(leading, axis, down)
        array = jnp.concatenate([before, array, after], axis=dim)
    return array


def slope(field_value):
    logistic = jax.nn.sigmoid(field_value)
    return logistic * (1.0 + field_value * (1.0 - logistic))


def pad_columns(field_value):
    return jnp.pad(field_value, ((0, 0), (0, 0), (1, 1), (0, 0)))


def shifted(padded, row_offset, col_offset, row_count, rim_start):
    col_count = padded.shape[2] - 2
    return padded[
        :,
        rim_start - row_offset : rim_start - row_offset + row_count,
        1 - col_offset : 1 - col_offset + col_count,
        :,
    ]


def weight_terms(left_field, padded, rim_start):
    row_count = left_field.shape[1]
    tap_list = []
    for row_offset in (-1, 0, 1):
        for col_offset in (-1, 0, 1):
            shifted_piece = shifted(padded, row_offset, col_offset, row_count, rim_start)
            tap_list.append(
                lax.dot_general(
                    left_field,
                    shifted_piece,
                    (((0, 1, 2), (0, 1, 2)), ((), ())),
                    preferred_element_type=jnp.float32,
                )
            )
    stacked = jnp.stack(tap_list)
    return stacked.reshape(-1, stacked.shape[2])


def back_terms(padded, weight, row_count, rim_start):
    accumulated = None
    for row_offset in (-1, 0, 1):
        for col_offset in (-1, 0, 1):
            shifted_piece = shifted(padded, row_offset, col_offset, row_count, rim_start)
            product = lax.dot_general(
                shifted_piece,
                weight[row_offset + 1, col_offset + 1],
                (((3,), (1,)), ((), ())),
                preferred_element_type=jnp.float32,
            )
            accumulated = product if accumulated is None else accumulated + product
    return accumulated


def swap(array, axis, step):
    peers = lax.axis_size(axis)
    return lax.ppermute(array, axis, [(i, i ^ step) for i in range(peers)])


def halve_step(blocks, axis, bit, dim):
    own = (lax.axis_index(axis) >> bit) & 1
    keep = lax.dynamic_index_in_dim(blocks, own, axis=dim, keepdims=False)
    give = lax.dynamic_index_in_dim(blocks, 1 - own, axis=dim, keepdims=False)
    half = give.shape[0] // 2
    if half == 0:
        return keep + swap(give, axis, 1 << bit)
    got = [swap(give[:half], axis, 1 << bit), swap(give[half:], axis, 1 << bit)]
    return keep + jnp.concatenate(got, axis=0)


def settle_stages(grad_scale):
    dates, bands = lax.axis_size("date"), lax.axis_size("band")
    band_bits, date_bits = bands.bit_length() - 1, dates.bit_length() - 1
    stages = []

    def start(grad_term):
        rows, cols = grad_term.shape
        piece = rows // (dates * bands)
        blocks = grad_term.reshape((dates,) + (2,) * band_bits + (piece, cols))
        return halve_step(blocks, "band", 0, 1)

    stages.append((start, True))
    orders = [list(range(1, band_bits)), list(range(band_bits - 1, 0, -1))]

    def split(blocks):
        half = blocks.shape[0] // 2
        return (blocks[:half], blocks[half:])

    if band_bits > 1:
        stages.append((split, False))
    for step in range(band_bits - 1):

        def band_step(parts, step=step):
            moved = []
            for part, order in zip(parts, orders):
                bit = order[step]
                done = order[:step]
                left = [b for b in range(1, band_bits) if b not in done]
                moved.append(halve_step(part, "band", bit, 1 + left.index(bit)))
            return tuple(moved)

        stages.append((band_step, True))
    def to_dates(parts):
        return tuple(p.reshape((2,) * (date_bits - 1) + p.shape[-2:]) for p in parts)

    stages.append((to_dates, False))
    for bit in range(date_bits - 1):

        def low_step(parts, bit=bit):
            return tuple(halve_step(p, "date", bit, date_bits - 2 - bit) for p in parts)

        stages.append((low_step, True))

    def top_step(parts):
        blocks = jnp.stack(parts, axis=0)
        return halve_step(blocks, "date", date_bits - 1, 0)

    stages.append((top_step, True))
    stages.append((lambda block: block * grad_scale, False))
    if band_bits > 1:

        def gather_far(block):
            mine = lax.axis_index("band") >> 1
            count = 1 << (band_bits - 1)
            half = block.shape[0] // 2

            def fetch(m):
                parts = [block[:half], block[half:]]
                return jnp.concatenate([swap(p, "band", m << 1) for p in parts], axis=0)

            got = [block] + [fetch(m) for m in range(1, count)]
            placed = []
            for spot in range(count):
                owner = int(format(spot, "0%db" % (band_bits - 1))[::-1], 2)
                pick = got[0]
                for m in range(1, count):
                    pick = jnp.where((mine ^ m) == owner, got[m], pick)
                placed.append(pick)
            return jnp.stack(placed, axis=0).reshape((2,) * (band_bits - 1) + block.shape)

        stages.append((gather_far, True))

    def gather_near(block):
        other = swap(block, "band", 1)
        low = (lax.axis_index("band") & 1) == 0
        return jnp.stack([jnp.where(low, block, other), jnp.where(low, other, block)], axis=0)

    stages.append((gather_near, True))
    return stages


class Chain:
    def __init__(self, stages, state):
        self.stages, self.state, self.at = stages, state, 0

    def advance(self, count):
        while count > 0 and self.at < len(self.stages):
            stage, sends = self.stages[self.at]
            self.state = stage(self.state)
            self.at += 1
            count -= int(sends)

    def tie(self, value):
        self.state, value = lax.optimization_barrier((self.state, value))
        return value

    def finish(self, rows, cols):
        self.advance(len(self.stages))
        return self.state.reshape(rows, cols)


def tie_chains(first, second):
    first.state, second.state = lax.optimization_barrier((first.state, second.state))


def body(inputs, preact_one, preact_two, cotangent, weight_one, weight_two):
    row_count = inputs.shape[1]
    grad_scale = 1.0 / (inputs.shape[0] * lax.axis_size("date"))
    act_one = jax.nn.silu(preact_one.astype(jnp.float32)).astype(jnp.bfloat16)
    delta_two = (cotangent.astype(jnp.float32) * slope(preact_two.astype(jnp.float32))).astype(
        jnp.bfloat16
    )
    padded_two = pad_columns(extended(delta_two, (("band", 1),), 1))
    term_two = weight_terms(act_one, padded_two, 1)
    out_rows = term_two.shape[0] // lax.axis_size("date")
    back_one = back_terms(padded_two, weight_two, row_count, 1)
    delta_one = (back_one * slope(preact_one.astype(jnp.float32))).astype(jnp.bfloat16)
    padded_one = pad_columns(extended(delta_one, (("band", 1),), 1))
    term_one = weight_terms(inputs, padded_one, 1)
    input_grad = back_terms(padded_one, weight_one, row_count, 1).astype(jnp.bfloat16)
    band_sends = lax.axis_size("band").bit_length() - 1
    date_sends = lax.axis_size("date").bit_length() - 1
    two = Chain(settle_stages(grad_scale), term_two)
    one = Chain(settle_stages(grad_scale), term_one)
    two.advance(band_sends)
    one.advance(1)
    tie_chains(two, one)
    two.advance(date_sends)
    one.advance(band_sends - 1)
    tie_chains(two, one)
    grad_two = two.finish(out_rows, term_two.shape[1])
    grad_one = one.finish(out_rows, term_one.shape[1])
    return (input_grad, grad_one, grad_two)


def solution(mesh):
    placed = (
        P("date", "band", None, None),
        P("date", "band", None, None),
        P("date", "band", None, None),
        P("date", "band", None, None),
        P(),
        P(),
    )
    return jax.shard_map(
        body,
        mesh=mesh,
        in_specs=placed,
        out_specs=(P("date", "band", None, None), P("date", None), P("date", None)),
        check_vma=False,
    )
```
